32 devices in a mesh: elem: 4 (over y, x), grp: 8 (over z, core).
Axes of the slice: x: 2, y: 2, z: 4, core: 2. Of those that a mesh axis runs over, the one named last changes fastest.
Arguments:
- params: bfloat16 [12, 32768], P(None, ('elem', 'grp')), may hold values from -0.796875 to 1
- profiles: bfloat16 [32768, 512], P(('elem', 'grp')), may hold values from 0 to 2
- weights: bfloat16 [32768], P(('elem', 'grp')), may hold values from 0.099609375 to 1
- destinations: int32 [32768], P(('elem', 'grp')), may hold values from 0 to 3, as said below
- table: int32 [1024, 12], replicated, may hold values from 0 to 3
Outputs:
- gram: float32 [4, 1024, 1024], P('elem', 'grp')
- moment: float32 [4, 1024, 512], P('elem', 'grp')
The draws below stay inside these ranges and needn't reach their ends.
Inputs may be any that keep to these rules, and one draw needn't show every extreme that they name: `destinations`: of the 1024 samples of one device at most 512 name one element. For every index of grp, one element drawn from the seed is named by exactly 512 samples of each of the 4 devices with that index.
All inputs are finite; a program needn't handle non-finite values.
Results may differ from the reference program's by a relative error of at most 0.0039.
Values may be sent and summed in bfloat16 or wider, within the bound.
No kernel may reach another device: no remote copies, remote signals or barrier semaphores. Data moves between devices by JAX's collectives and lax.ppermute only.
A program may use at most 128 MiB of HBM per device.

```python
import math
import jax
import jax.numpy as jnp
from jax import lax

P_SIZE = 1024
Q = 512
NPAR = 12
LEVELS = 4
S_DEV = 1024
CAP = 512
TOTAL = 32768
N_ELEM = 4
N_GRP = 8


def draw_destinations(key, part):
    blocks = N_ELEM * N_GRP
    favored = jax.random.randint(jax.random.fold_in(key, 11), (N_GRP,), 0, N_ELEM)
    favored_rows = jnp.tile(favored, N_ELEM)
    others = jax.random.randint(jax.random.fold_in(key, 12), (blocks, S_DEV - CAP), 0, N_ELEM - 1)
    others = others + (others >= favored_rows[:, None]).astype(jnp.int32)
    filled = jnp.broadcast_to(favored_rows[:, None], (blocks, CAP))
    labels = jnp.concatenate([filled, others], axis=1).astype(jnp.int32)
    labels = jax.random.permutation(jax.random.fold_in(key, 13), labels, axis=1, independent=True)
    return labels.reshape(-1).astype(jnp.int32)


def with_ends(array, own_key, least, high):
    extent = array.shape
    spot = [jax.random.randint(jax.random.fold_in(own_key, axis), (), 0, extent[axis]) for axis in range(len(extent))]
    array = array.at[tuple(spot)].set(least)
    longest = extent.index(max(extent))
    spot[longest] = (spot[longest] + 1) % extent[longest]
    return array.at[tuple(spot)].set(high)


def levels(stream_key, dims, pieces, smallest, largest):
    loudness, own = 1.0, jax.random.fold_in(stream_key, 6)
    for axis_at, blocks in pieces:
        steps = jnp.exp(jax.random.uniform(jax.random.fold_in(own, axis_at), (blocks,), jnp.float32, smallest / len(pieces), largest / len(pieces)))
        loudness = loudness * jnp.repeat(steps, dims[axis_at] // blocks).reshape([-1 if axis == axis_at else 1 for axis in range(len(dims))])
    return loudness


def setup_inputs(seed: int = 0) -> dict:
    seeds = jax.random.split(jax.random.key(seed), 6)
    return {
        "params": jnp.clip(-0.796875 + 1.796875 * jax.random.uniform(seeds[0], (NPAR, TOTAL), jnp.float32) ** levels(seeds[0], (NPAR, TOTAL), ((1, 32),), -0.2, 0.2), -0.796875, 1.0).astype(jnp.bfloat16),
        "profiles": jnp.clip(2.0 * jax.random.uniform(seeds[1], (TOTAL, Q), jnp.float32) ** levels(seeds[1], (TOTAL, Q), ((0, 32),), -0.2, 0.2), 0.0, 2.0).astype(jnp.bfloat16),
        "weights": jnp.clip(jnp.exp(math.log(1.0) - 2.306499 * jax.random.uniform(seeds[2], (TOTAL,), jnp.float32) ** levels(seeds[2], (TOTAL,), ((0, 32),), -0.2, 0.2)), 0.099609375, 1.0).astype(jnp.bfloat16),
        "destinations": draw_destinations(jax.random.fold_in(seeds[5], 71), 0),
        "table": with_ends(jax.random.randint(seeds[4], (P_SIZE, NPAR), 0, LEVELS), jax.random.fold_in(seeds[4], 1), 0, LEVELS - 1).astype(jnp.int32),
    }


def legendre_values(coords):
    first = jnp.ones_like(coords)
    second = coords
    values = [first, second]
    for degree in range(1, LEVELS - 1):
        nxt = ((2.0 * degree + 1.0) * coords * values[-1] - degree * values[-2]) / (degree + 1.0)
        values.append(nxt)
    scaled = [values[degree] * jnp.sqrt(2.0 * degree + 1.0) for degree in range(LEVELS)]
    return jnp.stack(scaled[:LEVELS], axis=1)

def evaluate_basis(coords_low, table):
    coords = coords_low.astype(jnp.float32)
    values = legendre_values(coords)
    levels_row = jnp.arange(LEVELS, dtype=jnp.int32)
    onehot = (table.T[:, None, :] == levels_row[None, :, None]).astype(jnp.float32)
    result = jnp.ones((coords.shape[1], table.shape[0]), jnp.float32)
    for column in range(table.shape[1]):
        factor = lax.dot_general(values[column], onehot[column], (((0,), (0,)), ((), ())), precision=lax.Precision.HIGHEST)
        result = result * factor
    return result

def reference(params, profiles, weights, destinations, table):
    scale = 1.0 / (N_GRP * S_DEV)
    grams = []
    moments = []
    for element in range(N_ELEM):
        chosen = destinations == element
        count = jnp.sum(chosen.astype(jnp.int32))
        order = jnp.argsort(jnp.where(chosen, 0, 1).astype(jnp.int32), stable=True).astype(jnp.int32)
        order = jnp.concatenate([order, jnp.zeros((S_DEV,), jnp.int32)])
        blocks = (count + S_DEV - 1) // S_DEV

        def step(block, carry):
            gram_acc, moment_acc = carry
            start = (block * S_DEV).astype(jnp.int32)
            picked = lax.dynamic_slice_in_dim(order, start, S_DEV)
            valid = start + jnp.arange(S_DEV, dtype=jnp.int32) < count
            basis = evaluate_basis(params[:, picked], table)
            basis_low = basis.astype(jnp.bfloat16)
            sample_w = weights[picked].astype(jnp.float32) * valid.astype(jnp.float32)
            weighted = (sample_w[:, None] * basis).astype(jnp.bfloat16)
            gram_acc = gram_acc + jnp.dot(weighted.T, basis_low, preferred_element_type=jnp.float32)
            moment_acc = moment_acc + jnp.dot(weighted.T, profiles[picked], preferred_element_type=jnp.float32)
            return (gram_acc, moment_acc)
        start_state = (jnp.zeros((P_SIZE, P_SIZE), jnp.float32), jnp.zeros((P_SIZE, Q), jnp.float32))
        gram_e, moment_e = lax.fori_loop(0, blocks, step, start_state)
        grams.append(gram_e * scale)
        moments.append(moment_e * scale)
    return (jnp.stack(grams), jnp.stack(moments))
```

```python
import jax
import jax.numpy as jnp
from jax import lax
from jax.sharding import PartitionSpec as P

LEVELS = 4
GROUP = 3


def legendre_values(coords):
    first = jnp.ones_like(coords)
    values = [first, coords]
    for degree in range(1, LEVELS - 1):
        nxt = ((2.0 * degree + 1.0) * coords * values[-1] - degree * values[-2]) / (degree + 1.0)
        values.append(nxt)
    scaled = [values[degree] * jnp.sqrt(2.0 * degree + 1.0) for degree in range(LEVELS)]
    return jnp.stack(scaled[:LEVELS], axis=1)


def split3(x):
    hi = x.astype(jnp.bfloat16)
    rest = x - hi.astype(jnp.float32)
    mid = rest.astype(jnp.bfloat16)
    lo = (rest - mid.astype(jnp.float32)).astype(jnp.bfloat16)
    return jnp.concatenate([hi, mid, lo], axis=0)


def evaluate_basis(coords_low, table):
    coords = coords_low.astype(jnp.float32)
    values = legendre_values(coords)
    npar, samples = coords.shape
    result = None
    for start in range(0, npar, GROUP):
        cols = range(start, min(start + GROUP, npar))
        combos = jnp.ones((1, samples), jnp.float32)
        code = jnp.zeros((table.shape[0],), jnp.int32)
        for j in cols:
            combos = (combos[:, None, :] * values[j][None, :, :]).reshape(-1, samples)
            code = code * LEVELS + table[:, j]
        count = combos.shape[0]
        onehot = (code[None, :] == jnp.arange(count, dtype=jnp.int32)[:, None]).astype(jnp.bfloat16)
        rhs = jnp.concatenate([onehot] * 3, axis=0)
        factor = lax.dot_general(
            split3(combos), rhs, (((0,), (0,)), ((), ())), preferred_element_type=jnp.float32
        )
        result = factor if result is None else result * factor
    return result


def on_device(params, profiles, weights, destinations, table):
    groups = lax.axis_size("elem")
    members = lax.axis_size("grp")
    samples = destinations.shape[0]
    cap = samples // 2
    scale = 1.0 / (members * samples)

    mine = destinations[:, None] == jnp.arange(groups, dtype=jnp.int32)[None, :]
    idx = jnp.arange(samples, dtype=jnp.int32)
    earlier = (idx[:, None] > idx[None, :]).astype(jnp.bfloat16)
    counts = jnp.dot(earlier, mine.astype(jnp.bfloat16), preferred_element_type=jnp.float32)
    slot = jnp.sum(jnp.where(mine, counts, 0.0), axis=1).astype(jnp.int32)
    sel = mine.T[:, None, :] & (slot[None, None, :] == jnp.arange(cap, dtype=jnp.int32)[None, :, None])
    sel = sel.astype(jnp.bfloat16)

    meta = jnp.concatenate([params, weights[None, :]], axis=0)
    prof_c = jnp.einsum("eis,sq->eiq", sel, profiles, preferred_element_type=jnp.float32).astype(jnp.bfloat16)
    meta_c = jnp.einsum("eis,js->eji", sel, meta, preferred_element_type=jnp.float32).astype(jnp.bfloat16)

    prof_r = lax.all_to_all(prof_c, "elem", 0, 0, tiled=True)
    meta_r = lax.all_to_all(meta_c, "elem", 0, 0, tiled=True)

    npar = params.shape[0]
    prof_r = prof_r.reshape(groups * cap, -1)
    meta_r = jnp.transpose(meta_r, (1, 0, 2)).reshape(npar + 1, groups * cap)
    basis = evaluate_basis(meta_r[:npar], table)
    sample_w = meta_r[npar].astype(jnp.float32)
    weighted = (sample_w[:, None] * basis).astype(jnp.bfloat16)
    rhs = jnp.concatenate([basis.astype(jnp.bfloat16), prof_r], axis=1)
    part = lax.dot_general(weighted, rhs, (((0,), (0,)), ((), ())), preferred_element_type=jnp.float32)
    rows = lax.psum_scatter(part, "grp", scatter_dimension=0, tiled=True) * scale
    width = table.shape[0]
    return (rows[None, :, :width], rows[None, :, width:])


def solution(mesh):
    in_specs = (
        P(None, ("elem", "grp")),
        P(("elem", "grp"), None),
        P(("elem", "grp")),
        P(("elem", "grp")),
        P(),
    )
    out_specs = (P("elem", "grp", None), P("elem", "grp", None))
    return jax.shard_map(
        on_device, mesh=mesh, in_specs=in_specs, out_specs=out_specs, check_vma=False
    )
```

```python
import jax
import jax.numpy as jnp
from jax import lax
from jax.sharding import PartitionSpec as P
from jax.experimental import pallas as pl
from jax.experimental.pallas import tpu as pltpu

LEVELS = 4
GROUP = 3


def legendre_values(coords):
    first = jnp.ones_like(coords)
    values = [first, coords]
    for degree in range(1, LEVELS - 1):
        nxt = ((2.0 * degree + 1.0) * coords * values[-1] - degree * values[-2]) / (degree + 1.0)
        values.append(nxt)
    scaled = [values[degree] * jnp.sqrt(2.0 * degree + 1.0) for degree in range(LEVELS)]
    return jnp.stack(scaled[:LEVELS], axis=1)


def split3(x):
    hi = x.astype(jnp.bfloat16)
    rest = x - hi.astype(jnp.float32)
    mid = rest.astype(jnp.bfloat16)
    lo = (rest - mid.astype(jnp.float32)).astype(jnp.bfloat16)
    return jnp.concatenate([hi, mid, lo], axis=0)


def group_tables(coords_low, table):
    coords = coords_low.astype(jnp.float32)
    values = legendre_values(coords)
    npar, samples = coords.shape
    width = LEVELS ** GROUP
    lhs = []
    rhs = []
    for start in range(0, npar, GROUP):
        cols = range(start, min(start + GROUP, npar))
        combos = jnp.ones((1, samples), jnp.float32)
        code = jnp.zeros((table.shape[0],), jnp.int32)
        for j in cols:
            combos = (combos[:, None, :] * values[j][None, :, :]).reshape(-1, samples)
            code = code * LEVELS + table[:, j]
        combos = jnp.pad(combos, ((0, width - combos.shape[0]), (0, 0)))
        onehot = (code[:, None] == jnp.arange(width, dtype=jnp.int32)[None, :]).astype(jnp.bfloat16)
        lhs.append(split3(combos))
        rhs.append(jnp.concatenate([onehot] * 3, axis=1))
    return jnp.stack(lhs), jnp.stack(rhs)


def partial_kernel(g_ref, oh_ref, w_ref, pr_ref, out_ref):
    @pl.when(pl.program_id(0) == 0)
    def _():
        out_ref[...] = jnp.zeros_like(out_ref)

    groups = g_ref.shape[0]
    basis = jnp.dot(oh_ref[0], g_ref[0], preferred_element_type=jnp.float32)
    for g in range(1, groups):
        basis = basis * jnp.dot(oh_ref[g], g_ref[g], preferred_element_type=jnp.float32)
    weighted = (w_ref[...] * basis).astype(jnp.bfloat16)
    low = basis.astype(jnp.bfloat16)
    terms = basis.shape[0]
    out_ref[:, :terms] += lax.dot_general(
        weighted, low, (((1,), (1,)), ((), ())), preferred_element_type=jnp.float32
    )
    out_ref[:, terms:] += jnp.dot(weighted, pr_ref[...], preferred_element_type=jnp.float32)


def partial_sums(lhs, rhs, sample_w, profiles, block=256):
    groups, width3, samples = lhs.shape
    terms = rhs.shape[1]
    q = profiles.shape[1]
    return pl.pallas_call(
        partial_kernel,
        grid=(samples // block,),
        in_specs=[
            pl.BlockSpec((groups, width3, block), lambda i: (0, 0, i)),
            pl.BlockSpec((groups, terms, width3), lambda i: (0, 0, 0)),
            pl.BlockSpec((1, block), lambda i: (0, i)),
            pl.BlockSpec((block, q), lambda i: (i, 0)),
        ],
        out_specs=pl.BlockSpec((terms, terms + q), lambda i: (0, 0)),
        out_shape=jax.ShapeDtypeStruct((terms, terms + q), jnp.float32),
        compiler_params=pltpu.CompilerParams(
            dimension_semantics=("arbitrary",), vmem_limit_bytes=48 * 1024 * 1024
        ),
    )(lhs, rhs, sample_w, profiles)


def on_device(params, profiles, weights, destinations, table):
    groups = lax.axis_size("elem")
    members = lax.axis_size("grp")
    samples = destinations.shape[0]
    cap = samples // 2
    scale = 1.0 / (members * samples)

    mine = destinations[:, None] == jnp.arange(groups, dtype=jnp.int32)[None, :]
    idx = jnp.arange(samples, dtype=jnp.int32)
    earlier = (idx[:, None] > idx[None, :]).astype(jnp.bfloat16)
    counts = jnp.dot(earlier, mine.astype(jnp.bfloat16), preferred_element_type=jnp.float32)
    slot = jnp.sum(jnp.where(mine, counts, 0.0), axis=1).astype(jnp.int32)
    sel = mine.T[:, None, :] & (slot[None, None, :] == jnp.arange(cap, dtype=jnp.int32)[None, :, None])
    sel = sel.astype(jnp.bfloat16)

    meta = jnp.concatenate([params, weights[None, :]], axis=0)
    prof_c = jnp.einsum("eis,sq->eiq", sel, profiles, preferred_element_type=jnp.float32).astype(jnp.bfloat16)
    meta_c = jnp.einsum("eis,js->eji", sel, meta, preferred_element_type=jnp.float32).astype(jnp.bfloat16)

    prof_r = lax.all_to_all(prof_c, "elem", 0, 0, tiled=True)
    meta_r = lax.all_to_all(meta_c, "elem", 0, 0, tiled=True)

    npar = params.shape[0]
    prof_r = prof_r.reshape(groups * cap, -1)
    meta_r = jnp.transpose(meta_r, (1, 0, 2)).reshape(npar + 1, groups * cap)
    lhs, rhs = group_tables(meta_r[:npar], table)
    sample_w = meta_r[npar:].astype(jnp.float32)
    part = partial_sums(lhs, rhs, sample_w, prof_r)
    rows = lax.psum_scatter(part, "grp", scatter_dimension=0, tiled=True) * scale
    width = table.shape[0]
    return (rows[None, :, :width], rows[None, :, width:])


def solution(mesh):
    in_specs = (
        P(None, ("elem", "grp")),
        P(("elem", "grp"), None),
        P(("elem", "grp")),
        P(("elem", "grp")),
        P(),
    )
    out_specs = (P("elem", "grp", None), P("elem", "grp", None))
    return jax.shard_map(
        on_device, mesh=mesh, in_specs=in_specs, out_specs=out_specs, check_vma=False
    )
```

```python
import numpy as np
import jax
import jax.numpy as jnp
from jax import lax
from jax.sharding import PartitionSpec as P
from jax.experimental import pallas as pl
from jax.experimental.pallas import tpu as pltpu

LEVELS = 4
GROUP = 3


def legendre_values(coords):
    first = jnp.ones_like(coords)
    values = [first, coords]
    for degree in range(1, LEVELS - 1):
        nxt = ((2.0 * degree + 1.0) * coords * values[-1] - degree * values[-2]) / (degree + 1.0)
        values.append(nxt)
    scaled = [values[degree] * jnp.sqrt(2.0 * degree + 1.0) for degree in range(LEVELS)]
    return jnp.stack(scaled[:LEVELS], axis=1)


def split3(x):
    hi = x.astype(jnp.bfloat16)
    rest = x - hi.astype(jnp.float32)
    mid = rest.astype(jnp.bfloat16)
    lo = (rest - mid.astype(jnp.float32)).astype(jnp.bfloat16)
    return jnp.concatenate([hi, mid, lo], axis=0)


def group_tables(coords_low, table):
    coords = coords_low.astype(jnp.float32)
    npar, samples = coords.shape
    first = jnp.ones_like(coords)
    values = [first, coords]
    for degree in range(1, LEVELS - 1):
        nxt = ((2.0 * degree + 1.0) * coords * values[-1] - degree * values[-2]) / (degree + 1.0)
        values.append(nxt)
    stacked = jnp.concatenate([values[d] * jnp.sqrt(2.0 * d + 1.0) for d in range(LEVELS)], axis=0)
    width = LEVELS ** GROUP
    n_groups = -(-npar // GROUP)
    pick = np.zeros((GROUP, n_groups * width, LEVELS * npar), np.float32)
    for g in range(n_groups):
        for c in range(width):
            for pos in range(GROUP):
                j = g * GROUP + pos
                degree = (c // LEVELS ** (GROUP - 1 - pos)) % LEVELS
                if j < npar:
                    pick[pos, g * width + c, degree * npar + j] = 1.0
                elif degree == 0:
                    pick[pos, g * width + c, 0] = 1.0
    pieces = split3(stacked)
    combos = None
    for pos in range(GROUP):
        select = jnp.asarray(np.concatenate([pick[pos]] * 3, axis=1), jnp.bfloat16)
        factor = jnp.dot(select, pieces, preferred_element_type=jnp.float32)
        combos = factor if combos is None else combos * factor
    rhs = []
    for start in range(0, n_groups * GROUP, GROUP):
        code = jnp.zeros((table.shape[0],), jnp.int32)
        for j in range(start, start + GROUP):
            code = code * LEVELS + (table[:, j] if j < npar else 0)
        onehot = (code[:, None] == jnp.arange(width, dtype=jnp.int32)[None, :]).astype(jnp.bfloat16)
        rhs.append(jnp.concatenate([onehot] * 3, axis=1))
    return combos.reshape(n_groups, width, samples), jnp.stack(rhs)


def partial_kernel(g_ref, oh_ref, w_ref, pr_ref, out_ref):
    @pl.when(pl.program_id(0) == 0)
    def _():
        out_ref[...] = jnp.zeros_like(out_ref)

    groups = g_ref.shape[0]
    basis = None
    for g in range(groups):
        factor = jnp.dot(oh_ref[g], split3(g_ref[g]), preferred_element_type=jnp.float32)
        basis = factor if basis is None else basis * factor
    weighted = (w_ref[...] * basis).astype(jnp.bfloat16)
    low = basis.astype(jnp.bfloat16)
    terms = basis.shape[0]
    out_ref[:, :terms] += lax.dot_general(
        weighted, low, (((1,), (1,)), ((), ())), preferred_element_type=jnp.float32
    )
    out_ref[:, terms:] += jnp.dot(weighted, pr_ref[...], preferred_element_type=jnp.float32)


def partial_sums(lhs, rhs, sample_w, profiles, block=256):
    groups, width, samples = lhs.shape
    terms = rhs.shape[1]
    q = profiles.shape[1]
    return pl.pallas_call(
        partial_kernel,
        grid=(samples // block,),
        in_specs=[
            pl.BlockSpec((groups, width, block), lambda i: (0, 0, i)),
            pl.BlockSpec((groups, terms, 3 * width), lambda i: (0, 0, 0)),
            pl.BlockSpec((1, block), lambda i: (0, i)),
            pl.BlockSpec((block, q), lambda i: (i, 0)),
        ],
        out_specs=pl.BlockSpec((terms, terms + q), lambda i: (0, 0)),
        out_shape=jax.ShapeDtypeStruct((terms, terms + q), jnp.float32),
        compiler_params=pltpu.CompilerParams(
            dimension_semantics=("arbitrary",), vmem_limit_bytes=48 * 1024 * 1024
        ),
    )(lhs, rhs, sample_w, profiles)


def on_device(params, profiles, weights, destinations, table):
    groups = lax.axis_size("elem")
    members = lax.axis_size("grp")
    samples = destinations.shape[0]
    cap = samples // 2
    scale = 1.0 / (members * samples)

    mine = destinations[:, None] == jnp.arange(groups, dtype=jnp.int32)[None, :]
    idx = jnp.arange(samples, dtype=jnp.int32)
    earlier = (idx[:, None] > idx[None, :]).astype(jnp.bfloat16)
    counts = jnp.dot(earlier, mine.astype(jnp.bfloat16), preferred_element_type=jnp.float32)
    slot = jnp.sum(jnp.where(mine, counts, 0.0), axis=1).astype(jnp.int32)
    sel = mine.T[:, None, :] & (slot[None, None, :] == jnp.arange(cap, dtype=jnp.int32)[None, :, None])
    sel = sel.astype(jnp.bfloat16)

    meta = jnp.concatenate([params, weights[None, :]], axis=0)
    prof_c = jnp.einsum("eis,sq->eiq", sel, profiles, preferred_element_type=jnp.float32).astype(jnp.bfloat16)
    meta_c = jnp.einsum("eis,js->eji", sel, meta, preferred_element_type=jnp.float32).astype(jnp.bfloat16)

    prof_r = lax.all_to_all(prof_c, "elem", 0, 0, tiled=True)
    meta_r = lax.all_to_all(meta_c, "elem", 0, 0, tiled=True)

    npar = params.shape[0]
    prof_r = prof_r.reshape(groups * cap, -1)
    meta_r = jnp.transpose(meta_r, (1, 0, 2)).reshape(npar + 1, groups * cap)
    lhs, rhs = group_tables(meta_r[:npar], table)
    sample_w = meta_r[npar:].astype(jnp.float32)
    part = partial_sums(lhs, rhs, sample_w, prof_r)
    rows = lax.psum_scatter(part, "grp", scatter_dimension=0, tiled=True) * scale
    width = table.shape[0]
    return (rows[None, :, :width], rows[None, :, width:])


def solution(mesh):
    in_specs = (
        P(None, ("elem", "grp")),
        P(("elem", "grp"), None),
        P(("elem", "grp")),
        P(("elem", "grp")),
        P(),
    )
    out_specs = (P("elem", "grp", None), P("elem", "grp", None))
    return jax.shard_map(
        on_device, mesh=mesh, in_specs=in_specs, out_specs=out_specs, check_vma=False
    )
```

```python
import functools

import numpy as np
import jax
import jax.numpy as jnp
from jax import lax
from jax.sharding import PartitionSpec as P
from jax.experimental import pallas as pl
from jax.experimental.pallas import tpu as pltpu

LEVELS = 4
GROUP = 3


def split3(x):
    hi = x.astype(jnp.bfloat16)
    rest = x - hi.astype(jnp.float32)
    mid = rest.astype(jnp.bfloat16)
    lo = (rest - mid.astype(jnp.float32)).astype(jnp.bfloat16)
    return jnp.concatenate([hi, mid, lo], axis=0)


def term_maps(table, rows):
    npar = table.shape[1]
    width = LEVELS ** GROUP
    n_groups = -(-npar // GROUP)
    maps = []
    for start in range(0, n_groups * GROUP, GROUP):
        code = jnp.zeros((table.shape[0],), jnp.int32)
        for j in range(start, start + GROUP):
            code = code * LEVELS + (table[:, j] if j < npar else 0)
        onehot = (code[:, None] == jnp.arange(width, dtype=jnp.int32)[None, :]).astype(jnp.bfloat16)
        maps.append(jnp.concatenate([onehot] * 3, axis=1))
    pick = np.zeros((GROUP, n_groups * width, 3 * LEVELS * rows), np.float32)
    for g in range(n_groups):
        for c in range(width):
            for pos in range(GROUP):
                j = g * GROUP + pos
                degree = (c // LEVELS ** (GROUP - 1 - pos)) % LEVELS
                col = degree * rows + j if j < npar else 0
                for piece in range(3):
                    pick[pos, g * width + c, piece * LEVELS * rows + col] = 1.0
    return jnp.stack(maps), jnp.asarray(pick, jnp.bfloat16)


def gram_kernel(m_ref, pick_ref, oh_ref, ohr_ref, gram_ref, *wt_refs, npar):
    @pl.when(pl.program_id(0) == 0)
    def _():
        gram_ref[...] = jnp.zeros_like(gram_ref)

    coords = m_ref[...].astype(jnp.float32)
    values = [jnp.ones_like(coords), coords]
    for degree in range(1, LEVELS - 1):
        nxt = ((2.0 * degree + 1.0) * coords * values[-1] - degree * values[-2]) / (degree + 1.0)
        values.append(nxt)
    stacked = jnp.concatenate(
        [values[d] * float(np.sqrt(np.float32(2 * d + 1))) for d in range(LEVELS)], axis=0
    )
    pieces = split3(stacked)
    combos = None
    for pos in range(pick_ref.shape[0]):
        factor = jnp.dot(pick_ref[pos], pieces, preferred_element_type=jnp.float32)
        combos = factor if combos is None else combos * factor
    groups = oh_ref.shape[0]
    width = combos.shape[0] // groups
    basis = None
    rows = None
    for g in range(groups):
        piece = split3(combos[g * width:(g + 1) * width])
        factor = jnp.dot(oh_ref[g], piece, preferred_element_type=jnp.float32)
        part = jnp.dot(ohr_ref[g], piece, preferred_element_type=jnp.float32)
        basis = factor if basis is None else basis * factor
        rows = part if rows is None else rows * part
    w = coords[npar:npar + 1]
    low = basis.astype(jnp.bfloat16)
    weighted_rows = (w * rows).astype(jnp.bfloat16)
    gram_ref[...] += lax.dot_general(
        weighted_rows, low, (((1,), (1,)), ((), ())), preferred_element_type=jnp.float32
    )
    if wt_refs:
        wt_refs[0][...] = (w * basis).astype(jnp.bfloat16)


def gram_rows(meta, pick, rhs, rhs_rows, npar, with_weighted, block=256):
    rows, samples = meta.shape
    groups, terms, width3 = rhs.shape
    picked = rhs_rows.shape[1]
    out_specs = [pl.BlockSpec((picked, terms), lambda i: (0, 0))]
    out_shape = [jax.ShapeDtypeStruct((picked, terms), jnp.float32)]
    if with_weighted:
        out_specs.append(pl.BlockSpec((terms, block), lambda i: (0, i)))
        out_shape.append(jax.ShapeDtypeStruct((terms, samples), jnp.bfloat16))
    return pl.pallas_call(
        functools.partial(gram_kernel, npar=npar),
        grid=(samples // block,),
        in_specs=[
            pl.BlockSpec((rows, block), lambda i: (0, i)),
            pl.BlockSpec(pick.shape, lambda i: (0, 0, 0)),
            pl.BlockSpec((groups, terms, width3), lambda i: (0, 0, 0)),
            pl.BlockSpec((groups, picked, width3), lambda i: (0, 0, 0)),
        ],
        out_specs=out_specs,
        out_shape=out_shape,
        compiler_params=pltpu.CompilerParams(
            dimension_semantics=("arbitrary",), vmem_limit_bytes=48 * 1024 * 1024
        ),
    )(meta, pick, rhs, rhs_rows)


def on_device(params, profiles, weights, destinations, table):
    groups = lax.axis_size("elem")
    members = lax.axis_size("grp")
    samples = destinations.shape[0]
    cap = samples // 2
    scale = 1.0 / (members * samples)

    mine = destinations[:, None] == jnp.arange(groups, dtype=jnp.int32)[None, :]
    idx = jnp.arange(samples, dtype=jnp.int32)
    earlier = (idx[:, None] > idx[None, :]).astype(jnp.bfloat16)
    counts = jnp.dot(earlier, mine.astype(jnp.bfloat16), preferred_element_type=jnp.float32)
    slot = jnp.sum(jnp.where(mine, counts, 0.0), axis=1).astype(jnp.int32)
    sel = mine.T[:, None, :] & (slot[None, None, :] == jnp.arange(cap, dtype=jnp.int32)[None, :, None])
    sel = sel.astype(jnp.bfloat16)

    prof_c = jnp.einsum("eis,sq->eiq", sel, profiles, preferred_element_type=jnp.float32).astype(jnp.bfloat16)
    prof_r = lax.all_to_all(prof_c, "elem", 0, 0, tiled=True)
    meta = jnp.concatenate([params, weights[None, :]], axis=0)
    meta_c = jnp.einsum("eis,js->eji", sel, meta, preferred_element_type=jnp.float32).astype(jnp.bfloat16)
    meta_r = lax.all_to_all(meta_c, "elem", 0, 0, tiled=True)

    npar = params.shape[0]
    q = profiles.shape[1]
    terms = table.shape[0]
    slots = groups * cap
    rows = -(-(npar + 1) // 16) * 16
    prof_r = prof_r.reshape(slots, q)
    meta_r = jnp.transpose(meta_r, (1, 0, 2)).reshape(npar + 1, slots)
    meta_r = jnp.pad(meta_r, ((0, rows - npar - 1), (0, 0)))

    me = lax.axis_index("grp")
    core = me % 2
    chip = me // 2
    pairs = members // 2
    own_rows = terms // members
    others = [
        lax.ppermute(meta_r, "grp", [(i, (i + 2 * k) % members) for i in range(members)])
        for k in range(1, pairs)
    ]
    rhs, pick = term_maps(table, rows)
    rhs_rows = lax.dynamic_slice_in_dim(rhs, chip * 2 * own_rows, 2 * own_rows, axis=1)
    gram_own, weighted_t = gram_rows(meta_r, pick, rhs, rhs_rows, npar, True)
    moment_part = jnp.dot(weighted_t, prof_r, preferred_element_type=jnp.float32)
    moment_rows = lax.psum_scatter(moment_part, "grp", scatter_dimension=0, tiled=True) * scale
    (gram_oth,) = gram_rows(jnp.concatenate(others, axis=1), pick, rhs, rhs_rows, npar, False)
    gram_chip = gram_own + gram_oth
    keep = lax.dynamic_slice_in_dim(gram_chip, core * own_rows, own_rows, axis=0)
    send = lax.dynamic_slice_in_dim(gram_chip, (1 - core) * own_rows, own_rows, axis=0)
    recv = lax.ppermute(send, "grp", [(i, i ^ 1) for i in range(members)])
    gram_out = (keep + recv) * scale
    return (gram_out[None], moment_rows[None])


def solution(mesh):
    in_specs = (
        P(None, ("elem", "grp")),
        P(("elem", "grp"), None),
        P(("elem", "grp")),
        P(("elem", "grp")),
        P(),
    )
    out_specs = (P("elem", "grp", None), P("elem", "grp", None))

    return jax.shard_map(on_device, mesh=mesh, in_specs=in_specs, out_specs=out_specs, check_vma=False)
```

```python
import functools

import numpy as np
import jax
import jax.numpy as jnp
from jax import lax
from jax.sharding import PartitionSpec as P
from jax.experimental import pallas as pl
from jax.experimental.pallas import tpu as pltpu

LEVELS = 4
GROUP = 3


def split3(x):
    hi = x.astype(jnp.bfloat16)
    rest = x - hi.astype(jnp.float32)
    mid = rest.astype(jnp.bfloat16)
    lo = (rest - mid.astype(jnp.float32)).astype(jnp.bfloat16)
    return jnp.concatenate([hi, mid, lo], axis=0)


def term_maps(table, rows):
    npar = table.shape[1]
    width = LEVELS ** GROUP
    n_groups = -(-npar // GROUP)
    maps = []
    for start in range(0, n_groups * GROUP, GROUP):
        code = jnp.zeros((table.shape[0],), jnp.int32)
        for j in range(start, start + GROUP):
            code = code * LEVELS + (table[:, j] if j < npar else 0)
        onehot = (code[:, None] == jnp.arange(width, dtype=jnp.int32)[None, :]).astype(jnp.bfloat16)
        maps.append(jnp.concatenate([onehot] * 3, axis=1))
    pick = np.zeros((GROUP, n_groups * width, 3 * LEVELS * rows), np.float32)
    for g in range(n_groups):
        for c in range(width):
            for pos in range(GROUP):
                j = g * GROUP + pos
                degree = (c // LEVELS ** (GROUP - 1 - pos)) % LEVELS
                col = degree * rows + j if j < npar else 0
                for piece in range(3):
                    pick[pos, g * width + c, piece * LEVELS * rows + col] = 1.0
    return jnp.stack(maps), jnp.asarray(pick, jnp.bfloat16)


def gram_kernel(m_ref, pick_ref, oh_ref, ohr_ref, gram_ref, *wt_refs, npar):
    @pl.when(pl.program_id(0) == 0)
    def _():
        gram_ref[...] = jnp.zeros_like(gram_ref)

    coords = m_ref[...].astype(jnp.float32)
    values = [jnp.ones_like(coords), coords]
    for degree in range(1, LEVELS - 1):
        nxt = ((2.0 * degree + 1.0) * coords * values[-1] - degree * values[-2]) / (degree + 1.0)
        values.append(nxt)
    stacked = jnp.concatenate(
        [values[d] * float(np.sqrt(np.float32(2 * d + 1))) for d in range(LEVELS)], axis=0
    )
    pieces = split3(stacked)
    combos = None
    for pos in range(pick_ref.shape[0]):
        factor = jnp.dot(pick_ref[pos], pieces, preferred_element_type=jnp.float32)
        combos = factor if combos is None else combos * factor
    groups = oh_ref.shape[0]
    width = combos.shape[0] // groups
    basis = None
    rows = None
    for g in range(groups):
        piece = split3(combos[g * width:(g + 1) * width])
        factor = jnp.dot(oh_ref[g], piece, preferred_element_type=jnp.float32)
        part = jnp.dot(ohr_ref[g], piece, preferred_element_type=jnp.float32)
        basis = factor if basis is None else basis * factor
        rows = part if rows is None else rows * part
    w = coords[npar:npar + 1]
    low = basis.astype(jnp.bfloat16)
    weighted_rows = (w * rows).astype(jnp.bfloat16)
    gram_ref[...] += lax.dot_general(
        weighted_rows, low, (((1,), (1,)), ((), ())), preferred_element_type=jnp.float32
    )
    if wt_refs:
        wt_refs[0][...] = (w * basis).astype(jnp.bfloat16)


def gram_rows(meta, pick, rhs, rhs_rows, npar, with_weighted, block=256):
    rows, samples = meta.shape
    groups, terms, width3 = rhs.shape
    picked = rhs_rows.shape[1]
    out_specs = [pl.BlockSpec((picked, terms), lambda i: (0, 0))]
    out_shape = [jax.ShapeDtypeStruct((picked, terms), jnp.float32)]
    if with_weighted:
        out_specs.append(pl.BlockSpec((terms, block), lambda i: (0, i)))
        out_shape.append(jax.ShapeDtypeStruct((terms, samples), jnp.bfloat16))
    return pl.pallas_call(
        functools.partial(gram_kernel, npar=npar),
        grid=(samples // block,),
        in_specs=[
            pl.BlockSpec((rows, block), lambda i: (0, i)),
            pl.BlockSpec(pick.shape, lambda i: (0, 0, 0)),
            pl.BlockSpec((groups, terms, width3), lambda i: (0, 0, 0)),
            pl.BlockSpec((groups, picked, width3), lambda i: (0, 0, 0)),
        ],
        out_specs=out_specs,
        out_shape=out_shape,
        compiler_params=pltpu.CompilerParams(
            dimension_semantics=("arbitrary",), vmem_limit_bytes=48 * 1024 * 1024
        ),
    )(meta, pick, rhs, rhs_rows)


def on_device(params, profiles, weights, destinations, table):
    groups = lax.axis_size("elem")
    members = lax.axis_size("grp")
    samples = destinations.shape[0]
    cap = samples // 2
    scale = 1.0 / (members * samples)

    mine = destinations[:, None] == jnp.arange(groups, dtype=jnp.int32)[None, :]
    idx = jnp.arange(samples, dtype=jnp.int32)
    earlier = (idx[:, None] > idx[None, :]).astype(jnp.bfloat16)
    counts = jnp.dot(earlier, mine.astype(jnp.bfloat16), preferred_element_type=jnp.float32)
    slot = jnp.sum(jnp.where(mine, counts, 0.0), axis=1).astype(jnp.int32)
    sel = mine.T[:, None, :] & (slot[None, None, :] == jnp.arange(cap, dtype=jnp.int32)[None, :, None])
    sel = sel.astype(jnp.bfloat16)

    prof_c = jnp.einsum("eis,sq->eiq", sel, profiles, preferred_element_type=jnp.float32).astype(jnp.bfloat16)
    prof_r = lax.all_to_all(prof_c, "elem", 0, 0, tiled=True)
    meta = jnp.concatenate([params, weights[None, :]], axis=0)
    meta_c = jnp.einsum("eis,js->eji", sel, meta, preferred_element_type=jnp.float32).astype(jnp.bfloat16)
    meta_r = lax.all_to_all(meta_c, "elem", 0, 0, tiled=True)

    npar = params.shape[0]
    q = profiles.shape[1]
    terms = table.shape[0]
    slots = groups * cap
    rows = -(-(npar + 1) // 16) * 16
    prof_r = prof_r.reshape(slots, q)
    meta_r = jnp.transpose(meta_r, (1, 0, 2)).reshape(npar + 1, slots)
    meta_r = jnp.pad(meta_r, ((0, rows - npar - 1), (0, 0)))

    me = lax.axis_index("grp")
    core = me % 2
    chip = me // 2
    pairs = members // 2
    own_rows = terms // members
    others = [
        lax.ppermute(meta_r, "grp", [(i, (i + 2 * k) % members) for i in range(members)])
        for k in range(1, pairs)
    ]
    rhs, pick = term_maps(table, rows)
    rhs_rows = lax.dynamic_slice_in_dim(rhs, chip * 2 * own_rows, 2 * own_rows, axis=1)
    gram_own, weighted_t = gram_rows(meta_r, pick, rhs, rhs_rows, npar, True)
    (gram_first,) = gram_rows(others[0], pick, rhs, rhs_rows, npar, False)
    gram_oth = gram_first
    moment_part = jnp.dot(weighted_t, prof_r, preferred_element_type=jnp.float32)
    moment_rows = lax.psum_scatter(moment_part, "grp", scatter_dimension=0, tiled=True) * scale
    if len(others) > 1:
        (gram_rest,) = gram_rows(jnp.concatenate(others[1:], axis=1), pick, rhs, rhs_rows, npar, False)
        gram_oth = gram_oth + gram_rest
    gram_chip = gram_own + gram_oth
    keep = lax.dynamic_slice_in_dim(gram_chip, core * own_rows, own_rows, axis=0)
    send = lax.dynamic_slice_in_dim(gram_chip, (1 - core) * own_rows, own_rows, axis=0)
    recv = lax.ppermute(send, "grp", [(i, i ^ 1) for i in range(members)])
    gram_out = (keep + recv) * scale
    return (gram_out[None], moment_rows[None])


def solution(mesh):
    in_specs = (
        P(None, ("elem", "grp")),
        P(("elem", "grp"), None),
        P(("elem", "grp")),
        P(("elem", "grp")),
        P(),
    )
    out_specs = (P("elem", "grp", None), P("elem", "grp", None))

    return jax.shard_map(on_device, mesh=mesh, in_specs=in_specs, out_specs=out_specs, check_vma=False)
```

```python
import functools

import numpy as np
import jax
import jax.numpy as jnp
from jax import lax
from jax.sharding import PartitionSpec as P
from jax.experimental import pallas as pl
from jax.experimental.pallas import tpu as pltpu

LEVELS = 4
GROUP = 3


def split3(x):
    hi = x.astype(jnp.bfloat16)
    rest = x - hi.astype(jnp.float32)
    mid = rest.astype(jnp.bfloat16)
    lo = (rest - mid.astype(jnp.float32)).astype(jnp.bfloat16)
    return jnp.concatenate([hi, mid, lo], axis=0)


def term_maps(table, rows):
    npar = table.shape[1]
    width = LEVELS ** GROUP
    n_groups = -(-npar // GROUP)
    maps = []
    for start in range(0, n_groups * GROUP, GROUP):
        code = jnp.zeros((table.shape[0],), jnp.int32)
        for j in range(start, start + GROUP):
            code = code * LEVELS + (table[:, j] if j < npar else 0)
        onehot = (code[:, None] == jnp.arange(width, dtype=jnp.int32)[None, :]).astype(jnp.bfloat16)
        maps.append(jnp.concatenate([onehot] * 3, axis=1))
    pick = np.zeros((GROUP, n_groups * width, 3 * LEVELS * rows), np.float32)
    for g in range(n_groups):
        for c in range(width):
            for pos in range(GROUP):
                j = g * GROUP + pos
                degree = (c // LEVELS ** (GROUP - 1 - pos)) % LEVELS
                col = degree * rows + j if j < npar else 0
                for piece in range(3):
                    pick[pos, g * width + c, piece * LEVELS * rows + col] = 1.0
    return jnp.stack(maps), jnp.asarray(pick, jnp.bfloat16)


def gram_kernel(m_ref, pick_ref, oh_ref, ohr_ref, gram_ref, *wt_refs, npar):
    @pl.when(pl.program_id(0) == 0)
    def _():
        gram_ref[...] = jnp.zeros_like(gram_ref)

    coords = m_ref[...].astype(jnp.float32)
    values = [jnp.ones_like(coords), coords]
    for degree in range(1, LEVELS - 1):
        nxt = ((2.0 * degree + 1.0) * coords * values[-1] - degree * values[-2]) / (degree + 1.0)
        values.append(nxt)
    stacked = jnp.concatenate(
        [values[d] * float(np.sqrt(np.float32(2 * d + 1))) for d in range(LEVELS)], axis=0
    )
    pieces = split3(stacked)
    combos = None
    for pos in range(pick_ref.shape[0]):
        factor = jnp.dot(pick_ref[pos], pieces, preferred_element_type=jnp.float32)
        combos = factor if combos is None else combos * factor
    groups = oh_ref.shape[0]
    width = combos.shape[0] // groups
    basis = None
    rows = None
    for g in range(groups):
        piece = split3(combos[g * width:(g + 1) * width])
        factor = jnp.dot(oh_ref[g], piece, preferred_element_type=jnp.float32)
        part = jnp.dot(ohr_ref[g], piece, preferred_element_type=jnp.float32)
        basis = factor if basis is None else basis * factor
        rows = part if rows is None else rows * part
    w = coords[npar:npar + 1]
    low = basis.astype(jnp.bfloat16)
    weighted_rows = (w * rows).astype(jnp.bfloat16)
    gram_ref[...] += lax.dot_general(
        weighted_rows, low, (((1,), (1,)), ((), ())), preferred_element_type=jnp.float32
    )
    if wt_refs:
        wt_refs[0][...] = (w * basis).astype(jnp.bfloat16)


def gram_rows(meta, pick, rhs, rhs_rows, npar, with_weighted, block=256):
    rows, samples = meta.shape
    groups, terms, width3 = rhs.shape
    picked = rhs_rows.shape[1]
    out_specs = [pl.BlockSpec((picked, terms), lambda i: (0, 0))]
    out_shape = [jax.ShapeDtypeStruct((picked, terms), jnp.float32)]
    if with_weighted:
        out_specs.append(pl.BlockSpec((terms, block), lambda i: (0, i)))
        out_shape.append(jax.ShapeDtypeStruct((terms, samples), jnp.bfloat16))
    return pl.pallas_call(
        functools.partial(gram_kernel, npar=npar),
        grid=(samples // block,),
        in_specs=[
            pl.BlockSpec((rows, block), lambda i: (0, i)),
            pl.BlockSpec(pick.shape, lambda i: (0, 0, 0)),
            pl.BlockSpec((groups, terms, width3), lambda i: (0, 0, 0)),
            pl.BlockSpec((groups, picked, width3), lambda i: (0, 0, 0)),
        ],
        out_specs=out_specs,
        out_shape=out_shape,
        compiler_params=pltpu.CompilerParams(
            dimension_semantics=("arbitrary",), vmem_limit_bytes=48 * 1024 * 1024
        ),
    )(meta, pick, rhs, rhs_rows)


def moment_kernel(w_ref, p_ref, o_ref, *, scale):
    o_ref[...] = jnp.dot(w_ref[...], p_ref[...], preferred_element_type=jnp.float32) * scale


def moment_sums(weighted_t, profiles, scale, block=256):
    terms, samples = weighted_t.shape
    q = profiles.shape[1]
    return pl.pallas_call(
        functools.partial(moment_kernel, scale=scale),
        grid=(terms // block,),
        in_specs=[
            pl.BlockSpec((block, samples), lambda i: (i, 0)),
            pl.BlockSpec((samples, q), lambda i: (0, 0)),
        ],
        out_specs=pl.BlockSpec((block, q), lambda i: (i, 0)),
        out_shape=jax.ShapeDtypeStruct((terms, q), jnp.float32),
        compiler_params=pltpu.CompilerParams(
            dimension_semantics=("arbitrary",), vmem_limit_bytes=48 * 1024 * 1024
        ),
    )(weighted_t, profiles)


def on_device(params, profiles, weights, destinations, table):
    groups = lax.axis_size("elem")
    members = lax.axis_size("grp")
    samples = destinations.shape[0]
    cap = samples // 2
    scale = 1.0 / (members * samples)

    mine = destinations[:, None] == jnp.arange(groups, dtype=jnp.int32)[None, :]
    idx = jnp.arange(samples, dtype=jnp.int32)
    earlier = (idx[:, None] > idx[None, :]).astype(jnp.bfloat16)
    counts = jnp.dot(earlier, mine.astype(jnp.bfloat16), preferred_element_type=jnp.float32)
    slot = jnp.sum(jnp.where(mine, counts, 0.0), axis=1).astype(jnp.int32)
    sel = mine.T[:, None, :] & (slot[None, None, :] == jnp.arange(cap, dtype=jnp.int32)[None, :, None])
    sel = sel.astype(jnp.bfloat16)

    prof_c = jnp.einsum("eis,sq->eiq", sel, profiles, preferred_element_type=jnp.float32).astype(jnp.bfloat16)
    prof_r = lax.all_to_all(prof_c, "elem", 0, 0, tiled=True)
    meta = jnp.concatenate([params, weights[None, :]], axis=0)
    meta_c = jnp.einsum("eis,js->eji", sel, meta, preferred_element_type=jnp.float32).astype(jnp.bfloat16)
    meta_r = lax.all_to_all(meta_c, "elem", 0, 0, tiled=True)

    npar = params.shape[0]
    q = profiles.shape[1]
    terms = table.shape[0]
    slots = groups * cap
    rows = -(-(npar + 1) // 16) * 16
    prof_r = prof_r.reshape(slots, q)
    meta_r = jnp.transpose(meta_r, (1, 0, 2)).reshape(npar + 1, slots)
    meta_r = jnp.pad(meta_r, ((0, rows - npar - 1), (0, 0)))

    me = lax.axis_index("grp")
    core = me % 2
    chip = me // 2
    pairs = members // 2
    own_rows = terms // members
    others = [
        lax.ppermute(meta_r, "grp", [(i, (i + 2 * k) % members) for i in range(members)])
        for k in range(1, pairs)
    ]
    rhs, pick = term_maps(table, rows)
    rhs_rows = lax.dynamic_slice_in_dim(rhs, chip * 2 * own_rows, 2 * own_rows, axis=1)
    gram_own, weighted_t = gram_rows(meta_r, pick, rhs, rhs_rows, npar, True)
    (gram_first,) = gram_rows(others[0], pick, rhs, rhs_rows, npar, False)
    gram_oth = gram_first
    moment_part = moment_sums(weighted_t, prof_r, scale)
    moment_rows = lax.psum_scatter(moment_part, "grp", scatter_dimension=0, tiled=True)
    if len(others) > 1:
        (gram_rest,) = gram_rows(jnp.concatenate(others[1:], axis=1), pick, rhs, rhs_rows, npar, False)
        gram_oth = gram_oth + gram_rest
    gram_chip = gram_own + gram_oth
    keep = lax.dynamic_slice_in_dim(gram_chip, core * own_rows, own_rows, axis=0)
    send = lax.dynamic_slice_in_dim(gram_chip, (1 - core) * own_rows, own_rows, axis=0)
    recv = lax.ppermute(send, "grp", [(i, i ^ 1) for i in range(members)])
    gram_out = (keep + recv) * scale
    return (gram_out[None], moment_rows[None])


def solution(mesh):
    in_specs = (
        P(None, ("elem", "grp")),
        P(("elem", "grp"), None),
        P(("elem", "grp")),
        P(("elem", "grp")),
        P(),
    )
    out_specs = (P("elem", "grp", None), P("elem", "grp", None))

    return jax.shard_map(on_device, mesh=mesh, in_specs=in_specs, out_specs=out_specs, check_vma=False)
```

```python
import functools

import numpy as np
import jax
import jax.numpy as jnp
from jax import lax
from jax.sharding import PartitionSpec as P
from jax.experimental import pallas as pl
from jax.experimental.pallas import tpu as pltpu

LEVELS = 4
GROUP = 3


def split3(x):
    hi = x.astype(jnp.bfloat16)
    rest = x - hi.astype(jnp.float32)
    mid = rest.astype(jnp.bfloat16)
    lo = (rest - mid.astype(jnp.float32)).astype(jnp.bfloat16)
    return jnp.concatenate([hi, mid, lo], axis=0)


def term_maps(table, rows):
    npar = table.shape[1]
    width = LEVELS ** GROUP
    n_groups = -(-npar // GROUP)
    maps = []
    for start in range(0, n_groups * GROUP, GROUP):
        code = jnp.zeros((table.shape[0],), jnp.int32)
        for j in range(start, start + GROUP):
            code = code * LEVELS + (table[:, j] if j < npar else 0)
        onehot = (code[:, None] == jnp.arange(width, dtype=jnp.int32)[None, :]).astype(jnp.bfloat16)
        maps.append(jnp.concatenate([onehot] * 3, axis=1))
    pick = np.zeros((GROUP, n_groups * width, 3 * LEVELS * rows), np.float32)
    for g in range(n_groups):
        for c in range(width):
            for pos in range(GROUP):
                j = g * GROUP + pos
                degree = (c // LEVELS ** (GROUP - 1 - pos)) % LEVELS
                col = degree * rows + j if j < npar else 0
                for piece in range(3):
                    pick[pos, g * width + c, piece * LEVELS * rows + col] = 1.0
    return jnp.stack(maps), jnp.asarray(pick, jnp.bfloat16)


def gram_kernel(m_ref, pick_ref, oh_ref, ohr_ref, gram_ref, *wt_refs, npar):
    @pl.when(pl.program_id(0) == 0)
    def _():
        gram_ref[...] = jnp.zeros_like(gram_ref)

    coords = m_ref[...].astype(jnp.float32)
    values = [jnp.ones_like(coords), coords]
    for degree in range(1, LEVELS - 1):
        nxt = ((2.0 * degree + 1.0) * coords * values[-1] - degree * values[-2]) / (degree + 1.0)
        values.append(nxt)
    stacked = jnp.concatenate(
        [values[d] * float(np.sqrt(np.float32(2 * d + 1))) for d in range(LEVELS)], axis=0
    )
    pieces = split3(stacked)
    combos = None
    for pos in range(pick_ref.shape[0]):
        factor = jnp.dot(pick_ref[pos], pieces, preferred_element_type=jnp.float32)
        combos = factor if combos is None else combos * factor
    groups = oh_ref.shape[0]
    width = combos.shape[0] // groups
    basis = None
    rows = None
    for g in range(groups):
        piece = split3(combos[g * width:(g + 1) * width])
        factor = jnp.dot(oh_ref[g], piece, preferred_element_type=jnp.float32)
        part = jnp.dot(ohr_ref[g], piece, preferred_element_type=jnp.float32)
        basis = factor if basis is None else basis * factor
        rows = part if rows is None else rows * part
    w = coords[npar:npar + 1]
    low = basis.astype(jnp.bfloat16)
    weighted_rows = (w * rows).astype(jnp.bfloat16)
    gram_ref[...] += lax.dot_general(
        weighted_rows, low, (((1,), (1,)), ((), ())), preferred_element_type=jnp.float32
    )
    if wt_refs:
        wt_refs[0][...] = (w * basis).astype(jnp.bfloat16)


def gram_rows(meta, pick, rhs, rhs_rows, npar, with_weighted, block=256):
    rows, samples = meta.shape
    groups, terms, width3 = rhs.shape
    picked = rhs_rows.shape[1]
    out_specs = [pl.BlockSpec((picked, terms), lambda i: (0, 0))]
    out_shape = [jax.ShapeDtypeStruct((picked, terms), jnp.float32)]
    if with_weighted:
        out_specs.append(pl.BlockSpec((terms, block), lambda i: (0, i)))
        out_shape.append(jax.ShapeDtypeStruct((terms, samples), jnp.bfloat16))
    return pl.pallas_call(
        functools.partial(gram_kernel, npar=npar),
        grid=(samples // block,),
        in_specs=[
            pl.BlockSpec((rows, block), lambda i: (0, i)),
            pl.BlockSpec(pick.shape, lambda i: (0, 0, 0)),
            pl.BlockSpec((groups, terms, width3), lambda i: (0, 0, 0)),
            pl.BlockSpec((groups, picked, width3), lambda i: (0, 0, 0)),
        ],
        out_specs=out_specs,
        out_shape=out_shape,
        compiler_params=pltpu.CompilerParams(
            dimension_semantics=("arbitrary",), vmem_limit_bytes=48 * 1024 * 1024
        ),
    )(meta, pick, rhs, rhs_rows)


def moment_kernel(w_ref, p_ref, o_ref, *, scale):
    o_ref[...] = jnp.dot(w_ref[...], p_ref[...], preferred_element_type=jnp.float32) * scale


def moment_sums(weighted_t, profiles, scale, block=256):
    terms, samples = weighted_t.shape
    q = profiles.shape[1]
    return pl.pallas_call(
        functools.partial(moment_kernel, scale=scale),
        grid=(terms // block,),
        in_specs=[
            pl.BlockSpec((block, samples), lambda i: (i, 0)),
            pl.BlockSpec((samples, q), lambda i: (0, 0)),
        ],
        out_specs=pl.BlockSpec((block, q), lambda i: (i, 0)),
        out_shape=jax.ShapeDtypeStruct((terms, q), jnp.float32),
        compiler_params=pltpu.CompilerParams(
            dimension_semantics=("arbitrary",), vmem_limit_bytes=48 * 1024 * 1024
        ),
    )(weighted_t, profiles)


def on_device(params, profiles, weights, destinations, table):
    groups = lax.axis_size("elem")
    members = lax.axis_size("grp")
    samples = destinations.shape[0]
    cap = samples // 2
    scale = 1.0 / (members * samples)

    mine = destinations[:, None] == jnp.arange(groups, dtype=jnp.int32)[None, :]
    idx = jnp.arange(samples, dtype=jnp.int32)
    earlier = (idx[:, None] > idx[None, :]).astype(jnp.bfloat16)
    counts = jnp.dot(earlier, mine.astype(jnp.bfloat16), preferred_element_type=jnp.float32)
    slot = jnp.sum(jnp.where(mine, counts, 0.0), axis=1).astype(jnp.int32)
    sel = mine.T[:, None, :] & (slot[None, None, :] == jnp.arange(cap, dtype=jnp.int32)[None, :, None])
    sel = sel.astype(jnp.bfloat16)

    prof_c = jnp.einsum("eis,sq->eiq", sel, profiles, preferred_element_type=jnp.float32).astype(jnp.bfloat16)
    prof_r = lax.all_to_all(prof_c, "elem", 0, 0, tiled=True)
    meta = jnp.concatenate([params, weights[None, :]], axis=0)
    meta_c = jnp.einsum("eis,js->eji", sel, meta, preferred_element_type=jnp.float32).astype(jnp.bfloat16)
    meta_r = lax.all_to_all(meta_c, "elem", 0, 0, tiled=True)

    npar = params.shape[0]
    q = profiles.shape[1]
    terms = table.shape[0]
    slots = groups * cap
    rows = -(-(npar + 1) // 16) * 16
    prof_r = prof_r.reshape(slots, q)
    meta_r = jnp.transpose(meta_r, (1, 0, 2)).reshape(npar + 1, slots)
    meta_r = jnp.pad(meta_r, ((0, rows - npar - 1), (0, 0)))

    me = lax.axis_index("grp")
    core = me % 2
    chip = me // 2
    pairs = members // 2
    own_rows = terms // members
    others = [
        lax.ppermute(meta_r, "grp", [(i, (i + 2 * k) % members) for i in range(members)])
        for k in range(1, pairs)
    ]
    rhs, pick = term_maps(table, rows)
    rhs_rows = lax.dynamic_slice_in_dim(rhs, chip * 2 * own_rows, 2 * own_rows, axis=1)
    gram_own, weighted_t = gram_rows(meta_r, pick, rhs, rhs_rows, npar, True)
    moment_part = moment_sums(weighted_t, prof_r, scale)
    moment_rows = lax.psum_scatter(moment_part, "grp", scatter_dimension=0, tiled=True)
    (gram_oth,) = gram_rows(jnp.concatenate(others, axis=1), pick, rhs, rhs_rows, npar, False)
    gram_chip = gram_own + gram_oth
    keep = lax.dynamic_slice_in_dim(gram_chip, core * own_rows, own_rows, axis=0)
    send = lax.dynamic_slice_in_dim(gram_chip, (1 - core) * own_rows, own_rows, axis=0)
    recv = lax.ppermute(send, "grp", [(i, i ^ 1) for i in range(members)])
    gram_out = (keep + recv) * scale
    return (gram_out[None], moment_rows[None])


def solution(mesh):
    in_specs = (
        P(None, ("elem", "grp")),
        P(("elem", "grp"), None),
        P(("elem", "grp")),
        P(("elem", "grp")),
        P(),
    )
    out_specs = (P("elem", "grp", None), P("elem", "grp", None))

    return jax.shard_map(on_device, mesh=mesh, in_specs=in_specs, out_specs=out_specs, check_vma=False)
```

```python
import functools

import numpy as np
import jax
import jax.numpy as jnp
from jax import lax
from jax.sharding import PartitionSpec as P
from jax.experimental import pallas as pl
from jax.experimental.pallas import tpu as pltpu

LEVELS = 4
GROUP = 3


def split3(x):
    hi = x.astype(jnp.bfloat16)
    rest = x - hi.astype(jnp.float32)
    mid = rest.astype(jnp.bfloat16)
    lo = (rest - mid.astype(jnp.float32)).astype(jnp.bfloat16)
    return jnp.concatenate([hi, mid, lo], axis=0)


def term_maps(table, rows):
    npar = table.shape[1]
    width = LEVELS ** GROUP
    n_groups = -(-npar // GROUP)
    maps = []
    for start in range(0, n_groups * GROUP, GROUP):
        code = jnp.zeros((table.shape[0],), jnp.int32)
        for j in range(start, start + GROUP):
            code = code * LEVELS + (table[:, j] if j < npar else 0)
        onehot = (code[:, None] == jnp.arange(width, dtype=jnp.int32)[None, :]).astype(jnp.bfloat16)
        maps.append(jnp.concatenate([onehot] * 3, axis=1))
    pick = np.zeros((GROUP, n_groups * width, 3 * LEVELS * rows), np.float32)
    for g in range(n_groups):
        for c in range(width):
            for pos in range(GROUP):
                j = g * GROUP + pos
                degree = (c // LEVELS ** (GROUP - 1 - pos)) % LEVELS
                col = degree * rows + j if j < npar else 0
                for piece in range(3):
                    pick[pos, g * width + c, piece * LEVELS * rows + col] = 1.0
    return jnp.stack(maps), jnp.asarray(pick, jnp.bfloat16)


def gram_kernel(m_ref, pick_ref, oh_ref, ohr_ref, gram_ref, *wt_refs, npar):
    @pl.when(pl.program_id(0) == 0)
    def _():
        gram_ref[...] = jnp.zeros_like(gram_ref)

    coords = m_ref[...].astype(jnp.float32)
    values = [jnp.ones_like(coords), coords]
    for degree in range(1, LEVELS - 1):
        nxt = ((2.0 * degree + 1.0) * coords * values[-1] - degree * values[-2]) / (degree + 1.0)
        values.append(nxt)
    stacked = jnp.concatenate(
        [values[d] * float(np.sqrt(np.float32(2 * d + 1))) for d in range(LEVELS)], axis=0
    )
    pieces = split3(stacked)
    combos = None
    for pos in range(pick_ref.shape[0]):
        factor = jnp.dot(pick_ref[pos], pieces, preferred_element_type=jnp.float32)
        combos = factor if combos is None else combos * factor
    groups = oh_ref.shape[0]
    width = combos.shape[0] // groups
    basis = None
    rows = None
    for g in range(groups):
        piece = split3(combos[g * width:(g + 1) * width])
        factor = jnp.dot(oh_ref[g], piece, preferred_element_type=jnp.float32)
        part = jnp.dot(ohr_ref[g], piece, preferred_element_type=jnp.float32)
        basis = factor if basis is None else basis * factor
        rows = part if rows is None else rows * part
    w = coords[npar:npar + 1]
    low = basis.astype(jnp.bfloat16)
    weighted_rows = (w * rows).astype(jnp.bfloat16)
    gram_ref[...] += lax.dot_general(
        weighted_rows, low, (((1,), (1,)), ((), ())), preferred_element_type=jnp.float32
    )
    if wt_refs:
        wt_refs[0][...] = (w * basis).astype(jnp.bfloat16)


def gram_rows(meta, pick, rhs, rhs_rows, npar, with_weighted, block=256):
    rows, samples = meta.shape
    groups, terms, width3 = rhs.shape
    picked = rhs_rows.shape[1]
    out_specs = [pl.BlockSpec((picked, terms), lambda i: (0, 0))]
    out_shape = [jax.ShapeDtypeStruct((picked, terms), jnp.float32)]
    if with_weighted:
        out_specs.append(pl.BlockSpec((terms, block), lambda i: (0, i)))
        out_shape.append(jax.ShapeDtypeStruct((terms, samples), jnp.bfloat16))
    return pl.pallas_call(
        functools.partial(gram_kernel, npar=npar),
        grid=(samples // block,),
        in_specs=[
            pl.BlockSpec((rows, block), lambda i: (0, i)),
            pl.BlockSpec(pick.shape, lambda i: (0, 0, 0)),
            pl.BlockSpec((groups, terms, width3), lambda i: (0, 0, 0)),
            pl.BlockSpec((groups, picked, width3), lambda i: (0, 0, 0)),
        ],
        out_specs=out_specs,
        out_shape=out_shape,
        compiler_params=pltpu.CompilerParams(
            dimension_semantics=("arbitrary",), vmem_limit_bytes=48 * 1024 * 1024
        ),
    )(meta, pick, rhs, rhs_rows)


def moment_kernel(w_ref, p_ref, o_ref, *, scale):
    o_ref[...] = jnp.dot(w_ref[...], p_ref[...], preferred_element_type=jnp.float32) * scale


def moment_sums(weighted_t, profiles, scale, block=256):
    terms, samples = weighted_t.shape
    q = profiles.shape[1]
    return pl.pallas_call(
        functools.partial(moment_kernel, scale=scale),
        grid=(terms // block,),
        in_specs=[
            pl.BlockSpec((block, samples), lambda i: (i, 0)),
            pl.BlockSpec((samples, q), lambda i: (0, 0)),
        ],
        out_specs=pl.BlockSpec((block, q), lambda i: (i, 0)),
        out_shape=jax.ShapeDtypeStruct((terms, q), jnp.float32),
        compiler_params=pltpu.CompilerParams(
            dimension_semantics=("arbitrary",), vmem_limit_bytes=48 * 1024 * 1024
        ),
    )(weighted_t, profiles)


def exchange(blocks, groups):
    if groups & (groups - 1):
        return lax.all_to_all(blocks, "elem", 0, 0, tiled=True)
    me = lax.axis_index("elem")
    got = [lax.dynamic_index_in_dim(blocks, me, 0, keepdims=False)]
    for m in range(1, groups):
        send = lax.dynamic_index_in_dim(blocks, me ^ m, 0, keepdims=False)
        got.append(lax.ppermute(send, "elem", [(i, i ^ m) for i in range(groups)]))
    return jnp.stack(got)


def on_device(params, profiles, weights, destinations, table):
    groups = lax.axis_size("elem")
    members = lax.axis_size("grp")
    samples = destinations.shape[0]
    cap = samples // 2
    scale = 1.0 / (members * samples)

    mine = destinations[:, None] == jnp.arange(groups, dtype=jnp.int32)[None, :]
    idx = jnp.arange(samples, dtype=jnp.int32)
    earlier = (idx[:, None] > idx[None, :]).astype(jnp.bfloat16)
    counts = jnp.dot(earlier, mine.astype(jnp.bfloat16), preferred_element_type=jnp.float32)
    slot = jnp.sum(jnp.where(mine, counts, 0.0), axis=1).astype(jnp.int32)
    sel = mine.T[:, None, :] & (slot[None, None, :] == jnp.arange(cap, dtype=jnp.int32)[None, :, None])
    sel = sel.astype(jnp.bfloat16)

    prof_c = jnp.einsum("eis,sq->eiq", sel, profiles, preferred_element_type=jnp.float32).astype(jnp.bfloat16)
    meta = jnp.concatenate([params, weights[None, :]], axis=0)
    meta_c = jnp.einsum("eis,js->eji", sel, meta, preferred_element_type=jnp.float32).astype(jnp.bfloat16)
    meta_r = exchange(meta_c, groups)
    prof_r = exchange(prof_c, groups)

    npar = params.shape[0]
    q = profiles.shape[1]
    terms = table.shape[0]
    slots = groups * cap
    rows = -(-(npar + 1) // 16) * 16
    prof_r = prof_r.reshape(slots, q)
    meta_r = jnp.transpose(meta_r, (1, 0, 2)).reshape(npar + 1, slots)
    meta_r = jnp.pad(meta_r, ((0, rows - npar - 1), (0, 0)))

    me = lax.axis_index("grp")
    core = me % 2
    chip = me // 2
    pairs = members // 2
    own_rows = terms // members
    others = [
        lax.ppermute(meta_r, "grp", [(i, (i + 2 * k) % members) for i in range(members)])
        for k in range(1, pairs)
    ]
    rhs, pick = term_maps(table, rows)
    rhs_rows = lax.dynamic_slice_in_dim(rhs, chip * 2 * own_rows, 2 * own_rows, axis=1)
    gram_own, weighted_t = gram_rows(meta_r, pick, rhs, rhs_rows, npar, True)
    moment_part = moment_sums(weighted_t, prof_r, scale)
    moment_rows = lax.psum_scatter(moment_part, "grp", scatter_dimension=0, tiled=True)
    (gram_oth,) = gram_rows(jnp.concatenate(others, axis=1), pick, rhs, rhs_rows, npar, False)
    gram_chip = gram_own + gram_oth
    keep = lax.dynamic_slice_in_dim(gram_chip, core * own_rows, own_rows, axis=0)
    send = lax.dynamic_slice_in_dim(gram_chip, (1 - core) * own_rows, own_rows, axis=0)
    recv = lax.ppermute(send, "grp", [(i, i ^ 1) for i in range(members)])
    gram_out = (keep + recv) * scale
    return (gram_out[None], moment_rows[None])


def solution(mesh):
    in_specs = (
        P(None, ("elem", "grp")),
        P(("elem", "grp"), None),
        P(("elem", "grp")),
        P(("elem", "grp")),
        P(),
    )
    out_specs = (P("elem", "grp", None), P("elem", "grp", None))

    return jax.shard_map(on_device, mesh=mesh, in_specs=in_specs, out_specs=out_specs, check_vma=False)
```

```python
import functools

import numpy as np
import jax
import jax.numpy as jnp
from jax import lax
from jax.sharding import PartitionSpec as P
from jax.experimental import pallas as pl
from jax.experimental.pallas import tpu as pltpu

LEVELS = 4
GROUP = 3


def split3(x):
    hi = x.astype(jnp.bfloat16)
    rest = x - hi.astype(jnp.float32)
    mid = rest.astype(jnp.bfloat16)
    lo = (rest - mid.astype(jnp.float32)).astype(jnp.bfloat16)
    return jnp.concatenate([hi, mid, lo], axis=0)


def term_maps(table, rows):
    npar = table.shape[1]
    width = LEVELS ** GROUP
    n_groups = -(-npar // GROUP)
    codes = []
    for start in range(0, n_groups * GROUP, GROUP):
        code = jnp.zeros((table.shape[0],), jnp.int32)
        for j in range(start, start + GROUP):
            code = code * LEVELS + (table[:, j] if j < npar else 0)
        codes.append(code)
    pick = np.zeros((GROUP, n_groups * width, 3 * LEVELS * rows), np.float32)
    for g in range(n_groups):
        for c in range(width):
            for pos in range(GROUP):
                j = g * GROUP + pos
                degree = (c // LEVELS ** (GROUP - 1 - pos)) % LEVELS
                col = degree * rows + j if j < npar else 0
                for piece in range(3):
                    pick[pos, g * width + c, piece * LEVELS * rows + col] = 1.0
    return jnp.stack(codes)[:, :, None], jnp.asarray(pick, jnp.bfloat16)


def gram_kernel(row0_ref, *refs, npar, n_meta, per, picked, with_weighted):
    metas = refs[:n_meta]
    pick_ref, code_ref, gram_ref = refs[n_meta:n_meta + 3]
    wt_refs = refs[n_meta + 3:-1] if with_weighted else ()
    oh_ref = refs[-1]
    step = pl.program_id(0)
    groups, _, width3 = oh_ref.shape
    width = width3 // 3

    @pl.when(step == 0)
    def _():
        gram_ref[...] = jnp.zeros_like(gram_ref)
        lanes = lax.broadcasted_iota(jnp.int32, (1, width3), 1) % width
        for g in range(groups):
            oh_ref[g] = (code_ref[g] == lanes).astype(jnp.bfloat16)

    m = metas[0][...]
    for k in range(1, n_meta):
        m = jnp.where(step >= k * per, metas[k][...], m)
    coords = m.astype(jnp.float32)
    values = [jnp.ones_like(coords), coords]
    for degree in range(1, LEVELS - 1):
        nxt = ((2.0 * degree + 1.0) * coords * values[-1] - degree * values[-2]) / (degree + 1.0)
        values.append(nxt)
    stacked = jnp.concatenate(
        [values[d] * float(np.sqrt(np.float32(2 * d + 1))) for d in range(LEVELS)], axis=0
    )
    pieces = split3(stacked)
    combos = None
    for pos in range(pick_ref.shape[0]):
        factor = jnp.dot(pick_ref[pos], pieces, preferred_element_type=jnp.float32)
        combos = factor if combos is None else combos * factor
    row0 = pl.multiple_of(row0_ref[0], picked)
    basis = None
    rows = None
    for g in range(groups):
        piece = split3(combos[g * width:(g + 1) * width])
        factor = jnp.dot(oh_ref[g], piece, preferred_element_type=jnp.float32)
        part = jnp.dot(oh_ref[g, pl.ds(row0, picked), :], piece, preferred_element_type=jnp.float32)
        basis = factor if basis is None else basis * factor
        rows = part if rows is None else rows * part
    w = coords[npar:npar + 1]
    low = basis.astype(jnp.bfloat16)
    weighted_rows = (w * rows).astype(jnp.bfloat16)
    gram_ref[...] += lax.dot_general(
        weighted_rows, low, (((1,), (1,)), ((), ())), preferred_element_type=jnp.float32
    )
    if with_weighted:
        wt_refs[0][...] = (w * basis).astype(jnp.bfloat16)


def gram_rows(metas, pick, codes, row0, picked, npar, with_weighted, block=256):
    rows, samples = metas[0].shape
    per = samples // block
    n_meta = len(metas)
    groups, terms, _ = codes.shape
    width3 = 3 * LEVELS ** GROUP

    def meta_map(k):
        return lambda i, r: (0, jnp.clip(i - k * per, 0, per - 1))

    out_specs = [pl.BlockSpec((picked, terms), lambda i, r: (0, 0))]
    out_shape = [jax.ShapeDtypeStruct((picked, terms), jnp.float32)]
    if with_weighted:
        out_specs.append(pl.BlockSpec((terms, block), lambda i, r: (0, i)))
        out_shape.append(jax.ShapeDtypeStruct((terms, samples), jnp.bfloat16))
    grid_spec = pltpu.PrefetchScalarGridSpec(
        num_scalar_prefetch=1,
        grid=(n_meta * per,),
        in_specs=[pl.BlockSpec((rows, block), meta_map(k)) for k in range(n_meta)] + [
            pl.BlockSpec(pick.shape, lambda i, r: (0, 0, 0)),
            pl.BlockSpec(codes.shape, lambda i, r: (0, 0, 0)),
        ],
        out_specs=out_specs,
        scratch_shapes=[pltpu.VMEM((groups, terms, width3), jnp.bfloat16)],
    )
    kernel = functools.partial(
        gram_kernel, npar=npar, n_meta=n_meta, per=per, picked=picked, with_weighted=with_weighted
    )
    return pl.pallas_call(
        kernel,
        grid_spec=grid_spec,
        out_shape=out_shape,
        compiler_params=pltpu.CompilerParams(
            dimension_semantics=("arbitrary",), vmem_limit_bytes=48 * 1024 * 1024
        ),
    )(row0, *metas, pick, codes)


def moment_kernel(w_ref, p_ref, o_ref, *, scale):
    o_ref[...] = jnp.dot(w_ref[...], p_ref[...], preferred_element_type=jnp.float32) * scale


def moment_sums(weighted_t, profiles, scale, block=256):
    terms, samples = weighted_t.shape
    q = profiles.shape[1]
    return pl.pallas_call(
        functools.partial(moment_kernel, scale=scale),
        grid=(terms // block,),
        in_specs=[
            pl.BlockSpec((block, samples), lambda i: (i, 0)),
            pl.BlockSpec((samples, q), lambda i: (0, 0)),
        ],
        out_specs=pl.BlockSpec((block, q), lambda i: (i, 0)),
        out_shape=jax.ShapeDtypeStruct((terms, q), jnp.float32),
        compiler_params=pltpu.CompilerParams(
            dimension_semantics=("arbitrary",), vmem_limit_bytes=48 * 1024 * 1024
        ),
    )(weighted_t, profiles)


def exchange(blocks, groups):
    if groups & (groups - 1):
        return lax.all_to_all(blocks, "elem", 0, 0, tiled=True)
    me = lax.axis_index("elem")
    got = [lax.dynamic_index_in_dim(blocks, me, 0, keepdims=False)]
    for m in range(1, groups):
        send = lax.dynamic_index_in_dim(blocks, me ^ m, 0, keepdims=False)
        got.append(lax.ppermute(send, "elem", [(i, i ^ m) for i in range(groups)]))
    return jnp.stack(got)


def on_device(params, profiles, weights, destinations, table):
    groups = lax.axis_size("elem")
    members = lax.axis_size("grp")
    samples = destinations.shape[0]
    cap = samples // 2
    scale = 1.0 / (members * samples)

    mine = destinations[:, None] == jnp.arange(groups, dtype=jnp.int32)[None, :]
    idx = jnp.arange(samples, dtype=jnp.int32)
    earlier = (idx[:, None] > idx[None, :]).astype(jnp.bfloat16)
    counts = jnp.dot(earlier, mine.astype(jnp.bfloat16), preferred_element_type=jnp.float32)
    slot = jnp.sum(jnp.where(mine, counts, 0.0), axis=1).astype(jnp.int32)
    sel = mine.T[:, None, :] & (slot[None, None, :] == jnp.arange(cap, dtype=jnp.int32)[None, :, None])
    sel = sel.astype(jnp.bfloat16)

    prof_c = jnp.einsum("eis,sq->eiq", sel, profiles, preferred_element_type=jnp.float32).astype(jnp.bfloat16)
    npar = params.shape[0]
    rows = -(-(npar + 1) // 16) * 16
    meta = jnp.concatenate(
        [params, weights[None, :], jnp.zeros((rows - npar - 1, samples), params.dtype)], axis=0
    )
    meta_c = jnp.einsum("eis,js->eji", sel, meta, preferred_element_type=jnp.float32).astype(jnp.bfloat16)
    meta_r = exchange(meta_c, groups)
    prof_r = exchange(prof_c, groups)

    q = profiles.shape[1]
    terms = table.shape[0]
    slots = groups * cap
    prof_r = prof_r.reshape(slots, q)
    meta_r = jnp.transpose(meta_r, (1, 0, 2)).reshape(rows, slots)

    me = lax.axis_index("grp")
    core = me % 2
    chip = me // 2
    pairs = members // 2
    own_rows = terms // members
    others = [
        lax.ppermute(meta_r, "grp", [(i, (i + 2 * k) % members) for i in range(members)])
        for k in range(1, pairs)
    ]
    codes, pick = term_maps(table, rows)
    row0 = (chip * 2 * own_rows).astype(jnp.int32).reshape(1)
    gram_own, weighted_t = gram_rows([meta_r], pick, codes, row0, 2 * own_rows, npar, True)
    moment_part = moment_sums(weighted_t, prof_r, scale)
    moment_rows = lax.psum_scatter(moment_part, "grp", scatter_dimension=0, tiled=True)
    (gram_oth,) = gram_rows(others, pick, codes, row0, 2 * own_rows, npar, False)
    gram_chip = gram_own + gram_oth
    keep = lax.dynamic_slice_in_dim(gram_chip, core * own_rows, own_rows, axis=0)
    send = lax.dynamic_slice_in_dim(gram_chip, (1 - core) * own_rows, own_rows, axis=0)
    recv = lax.ppermute(send, "grp", [(i, i ^ 1) for i in range(members)])
    gram_out = (keep + recv) * scale
    return (gram_out[None], moment_rows[None])


def solution(mesh):
    in_specs = (
        P(None, ("elem", "grp")),
        P(("elem", "grp"), None),
        P(("elem", "grp")),
        P(("elem", "grp")),
        P(),
    )
    out_specs = (P("elem", "grp", None), P("elem", "grp", None))

    return jax.shard_map(on_device, mesh=mesh, in_specs=in_specs, out_specs=out_specs, check_vma=False)
```

```python
import functools

import numpy as np
import jax
import jax.numpy as jnp
from jax import lax
from jax.sharding import PartitionSpec as P
from jax.experimental import pallas as pl
from jax.experimental.pallas import tpu as pltpu

LEVELS = 4
GROUP = 3


def split3(x):
    hi = x.astype(jnp.bfloat16)
    rest = x - hi.astype(jnp.float32)
    mid = rest.astype(jnp.bfloat16)
    lo = (rest - mid.astype(jnp.float32)).astype(jnp.bfloat16)
    return jnp.concatenate([hi, mid, lo], axis=0)


def term_maps(table, rows):
    npar = table.shape[1]
    width = LEVELS ** GROUP
    n_groups = -(-npar // GROUP)
    codes = []
    for start in range(0, n_groups * GROUP, GROUP):
        code = jnp.zeros((table.shape[0],), jnp.int32)
        for j in range(start, start + GROUP):
            code = code * LEVELS + (table[:, j] if j < npar else 0)
        codes.append(code)
    pick = np.zeros((GROUP, n_groups * width, 3 * LEVELS * rows), np.float32)
    for g in range(n_groups):
        for c in range(width):
            for pos in range(GROUP):
                j = g * GROUP + pos
                degree = (c // LEVELS ** (GROUP - 1 - pos)) % LEVELS
                col = degree * rows + j if j < npar else 0
                for piece in range(3):
                    pick[pos, g * width + c, piece * LEVELS * rows + col] = 1.0
    return jnp.stack(codes)[:, :, None], jnp.asarray(pick, jnp.bfloat16)


def gram_kernel(row0_ref, *refs, npar, n_meta, per, picked, with_weighted):
    metas = refs[:n_meta]
    pick_ref, code_ref, gram_ref = refs[n_meta:n_meta + 3]
    wt_refs = refs[n_meta + 3:-1] if with_weighted else ()
    oh_ref = refs[-1]
    step = pl.program_id(0)
    groups, _, width3 = oh_ref.shape
    width = width3 // 3

    @pl.when(step == 0)
    def _():
        gram_ref[...] = jnp.zeros_like(gram_ref)
        lanes = lax.broadcasted_iota(jnp.int32, (1, width3), 1) % width
        for g in range(groups):
            oh_ref[g] = (code_ref[g] == lanes).astype(jnp.bfloat16)

    m = metas[0][...]
    for k in range(1, n_meta):
        m = jnp.where(step >= k * per, metas[k][...], m)
    coords = m.astype(jnp.float32)
    values = [jnp.ones_like(coords), coords]
    for degree in range(1, LEVELS - 1):
        nxt = ((2.0 * degree + 1.0) * coords * values[-1] - degree * values[-2]) / (degree + 1.0)
        values.append(nxt)
    stacked = jnp.concatenate(
        [values[d] * float(np.sqrt(np.float32(2 * d + 1))) for d in range(LEVELS)], axis=0
    )
    pieces = split3(stacked)
    combos = None
    for pos in range(pick_ref.shape[0]):
        factor = jnp.dot(pick_ref[pos], pieces, preferred_element_type=jnp.float32)
        combos = factor if combos is None else combos * factor
    row0 = pl.multiple_of(row0_ref[0], picked)
    basis = None
    rows = None
    for g in range(groups):
        piece = split3(combos[g * width:(g + 1) * width])
        factor = jnp.dot(oh_ref[g], piece, preferred_element_type=jnp.float32)
        part = jnp.dot(oh_ref[g, pl.ds(row0, picked), :], piece, preferred_element_type=jnp.float32)
        basis = factor if basis is None else basis * factor
        rows = part if rows is None else rows * part
    w = coords[npar:npar + 1]
    low = basis.astype(jnp.bfloat16)
    weighted_rows = (w * rows).astype(jnp.bfloat16)
    gram_ref[...] += lax.dot_general(
        weighted_rows, low, (((1,), (1,)), ((), ())), preferred_element_type=jnp.float32
    )
    if with_weighted:
        wt_refs[0][...] = (w * basis).astype(jnp.bfloat16)


def gram_rows(metas, pick, codes, row0, picked, npar, with_weighted, block=512):
    rows, samples = metas[0].shape
    per = samples // block
    n_meta = len(metas)
    groups, terms, _ = codes.shape
    width3 = 3 * LEVELS ** GROUP

    def meta_map(k):
        return lambda i, r: (0, jnp.clip(i - k * per, 0, per - 1))

    out_specs = [pl.BlockSpec((picked, terms), lambda i, r: (0, 0))]
    out_shape = [jax.ShapeDtypeStruct((picked, terms), jnp.float32)]
    if with_weighted:
        out_specs.append(pl.BlockSpec((terms, block), lambda i, r: (0, i)))
        out_shape.append(jax.ShapeDtypeStruct((terms, samples), jnp.bfloat16))
    grid_spec = pltpu.PrefetchScalarGridSpec(
        num_scalar_prefetch=1,
        grid=(n_meta * per,),
        in_specs=[pl.BlockSpec((rows, block), meta_map(k)) for k in range(n_meta)] + [
            pl.BlockSpec(pick.shape, lambda i, r: (0, 0, 0)),
            pl.BlockSpec(codes.shape, lambda i, r: (0, 0, 0)),
        ],
        out_specs=out_specs,
        scratch_shapes=[pltpu.VMEM((groups, terms, width3), jnp.bfloat16)],
    )
    kernel = functools.partial(
        gram_kernel, npar=npar, n_meta=n_meta, per=per, picked=picked, with_weighted=with_weighted
    )
    return pl.pallas_call(
        kernel,
        grid_spec=grid_spec,
        out_shape=out_shape,
        compiler_params=pltpu.CompilerParams(
            dimension_semantics=("arbitrary",), vmem_limit_bytes=48 * 1024 * 1024
        ),
    )(row0, *metas, pick, codes)


def moment_kernel(w_ref, *refs, scale):
    p_refs, o_ref = refs[:-1], refs[-1]
    cap = p_refs[0].shape[0]
    acc = None
    for k, p_ref in enumerate(p_refs):
        part = jnp.dot(w_ref[:, k * cap:(k + 1) * cap], p_ref[...], preferred_element_type=jnp.float32)
        acc = part if acc is None else acc + part
    o_ref[...] = acc * scale


def moment_sums(weighted_t, profiles, scale, block=256):
    terms, samples = weighted_t.shape
    cap, q = profiles[0].shape
    return pl.pallas_call(
        functools.partial(moment_kernel, scale=scale),
        grid=(terms // block,),
        in_specs=[pl.BlockSpec((block, samples), lambda i: (i, 0))]
        + [pl.BlockSpec((cap, q), lambda i: (0, 0)) for _ in profiles],
        out_specs=pl.BlockSpec((block, q), lambda i: (i, 0)),
        out_shape=jax.ShapeDtypeStruct((terms, q), jnp.float32),
        compiler_params=pltpu.CompilerParams(
            dimension_semantics=("arbitrary",), vmem_limit_bytes=48 * 1024 * 1024
        ),
    )(weighted_t, *profiles)


def exchange(blocks, groups):
    if groups & (groups - 1):
        got = lax.all_to_all(blocks, "elem", 0, 0, tiled=True)
        return [got[t] for t in range(groups)]
    got = [blocks[0]]
    for m in range(1, groups):
        got.append(lax.ppermute(blocks[m], "elem", [(i, i ^ m) for i in range(groups)]))
    return got


def partners(groups):
    if groups & (groups - 1):
        return jnp.arange(groups, dtype=jnp.int32)
    return lax.axis_index("elem") ^ jnp.arange(groups, dtype=jnp.int32)


def on_device(params, profiles, weights, destinations, table):
    groups = lax.axis_size("elem")
    members = lax.axis_size("grp")
    samples = destinations.shape[0]
    cap = samples // 2
    scale = 1.0 / (members * samples)

    mine = destinations[:, None] == partners(groups)[None, :]
    idx = jnp.arange(samples, dtype=jnp.int32)
    earlier = (idx[:, None] > idx[None, :]).astype(jnp.bfloat16)
    counts = jnp.dot(earlier, mine.astype(jnp.bfloat16), preferred_element_type=jnp.float32)
    slot = jnp.sum(jnp.where(mine, counts, 0.0), axis=1).astype(jnp.int32)
    sel = mine.T[:, None, :] & (slot[None, None, :] == jnp.arange(cap, dtype=jnp.int32)[None, :, None])
    sel = sel.astype(jnp.bfloat16)

    prof_c = jnp.einsum("eis,sq->eiq", sel, profiles, preferred_element_type=jnp.float32).astype(jnp.bfloat16)
    npar = params.shape[0]
    rows = -(-(npar + 1) // 16) * 16
    meta = jnp.concatenate(
        [params, weights[None, :], jnp.zeros((rows - npar - 1, samples), params.dtype)], axis=0
    )
    meta_c = jnp.einsum("eis,js->eji", sel, meta, preferred_element_type=jnp.float32).astype(jnp.bfloat16)
    meta_r = jnp.stack(exchange(meta_c, groups))
    prof_r = exchange(prof_c, groups)

    terms = table.shape[0]
    slots = groups * cap
    meta_r = jnp.transpose(meta_r, (1, 0, 2)).reshape(rows, slots)

    me = lax.axis_index("grp")
    core = me % 2
    chip = me // 2
    pairs = members // 2
    own_rows = terms // members
    others = [
        lax.ppermute(meta_r, "grp", [(i, (i + 2 * k) % members) for i in range(members)])
        for k in range(1, pairs)
    ]
    codes, pick = term_maps(table, rows)
    row0 = (chip * 2 * own_rows).astype(jnp.int32).reshape(1)
    gram_own, weighted_t = gram_rows([meta_r], pick, codes, row0, 2 * own_rows, npar, True)
    moment_part = moment_sums(weighted_t, prof_r, scale)
    moment_rows = lax.psum_scatter(moment_part, "grp", scatter_dimension=0, tiled=True)
    (gram_oth,) = gram_rows(others, pick, codes, row0, 2 * own_rows, npar, False)
    gram_chip = gram_own + gram_oth
    keep = lax.dynamic_slice_in_dim(gram_chip, core * own_rows, own_rows, axis=0)
    send = lax.dynamic_slice_in_dim(gram_chip, (1 - core) * own_rows, own_rows, axis=0)
    recv = lax.ppermute(send, "grp", [(i, i ^ 1) for i in range(members)])
    gram_out = (keep + recv) * scale
    return (gram_out[None], moment_rows[None])


def solution(mesh):
    in_specs = (
        P(None, ("elem", "grp")),
        P(("elem", "grp"), None),
        P(("elem", "grp")),
        P(("elem", "grp")),
        P(),
    )
    out_specs = (P("elem", "grp", None), P("elem", "grp", None))

    return jax.shard_map(on_device, mesh=mesh, in_specs=in_specs, out_specs=out_specs, check_vma=False)
```

```python
import functools

import numpy as np
import jax
import jax.numpy as jnp
from jax import lax
from jax.sharding import PartitionSpec as P
from jax.experimental import pallas as pl
from jax.experimental.pallas import tpu as pltpu

LEVELS = 4
GROUP = 3


def split3(x):
    hi = x.astype(jnp.bfloat16)
    rest = x - hi.astype(jnp.float32)
    mid = rest.astype(jnp.bfloat16)
    lo = (rest - mid.astype(jnp.float32)).astype(jnp.bfloat16)
    return jnp.concatenate([hi, mid, lo], axis=0)


def term_maps(table, rows):
    npar = table.shape[1]
    width = LEVELS ** GROUP
    n_groups = -(-npar // GROUP)
    codes = []
    for start in range(0, n_groups * GROUP, GROUP):
        code = jnp.zeros((table.shape[0],), jnp.int32)
        for j in range(start, start + GROUP):
            code = code * LEVELS + (table[:, j] if j < npar else 0)
        codes.append(code)
    pick = np.zeros((GROUP, n_groups * width, 3 * LEVELS * rows), np.float32)
    for g in range(n_groups):
        for c in range(width):
            for pos in range(GROUP):
                j = g * GROUP + pos
                degree = (c // LEVELS ** (GROUP - 1 - pos)) % LEVELS
                col = degree * rows + j if j < npar else 0
                for piece in range(3):
                    pick[pos, g * width + c, piece * LEVELS * rows + col] = 1.0
    return jnp.stack(codes)[:, :, None], jnp.asarray(pick, jnp.bfloat16)


def gram_kernel(row0_ref, *refs, npar, n_meta, per, picked, with_weighted):
    metas = refs[:n_meta]
    pick_ref, code_ref, gram_ref = refs[n_meta:n_meta + 3]
    wt_refs = refs[n_meta + 3:-1] if with_weighted else ()
    oh_ref = refs[-1]
    step = pl.program_id(0)
    groups, _, width3 = oh_ref.shape
    width = width3 // 3

    @pl.when(step == 0)
    def _():
        gram_ref[...] = jnp.zeros_like(gram_ref)
        lanes = lax.broadcasted_iota(jnp.int32, (1, width3), 1) % width
        for g in range(groups):
            oh_ref[g] = (code_ref[g] == lanes).astype(jnp.bfloat16)

    m = metas[0][...]
    for k in range(1, n_meta):
        m = jnp.where(step >= k * per, metas[k][...], m)
    coords = m.astype(jnp.float32)
    values = [jnp.ones_like(coords), coords]
    for degree in range(1, LEVELS - 1):
        nxt = ((2.0 * degree + 1.0) * coords * values[-1] - degree * values[-2]) / (degree + 1.0)
        values.append(nxt)
    stacked = jnp.concatenate(
        [values[d] * float(np.sqrt(np.float32(2 * d + 1))) for d in range(LEVELS)], axis=0
    )
    pieces = split3(stacked)
    combos = None
    for pos in range(pick_ref.shape[0]):
        factor = jnp.dot(pick_ref[pos], pieces, preferred_element_type=jnp.float32)
        combos = factor if combos is None else combos * factor
    row0 = pl.multiple_of(row0_ref[0], picked)
    basis = None
    rows = None
    for g in range(groups):
        piece = split3(combos[g * width:(g + 1) * width])
        factor = jnp.dot(oh_ref[g], piece, preferred_element_type=jnp.float32)
        part = jnp.dot(oh_ref[g, pl.ds(row0, picked), :], piece, preferred_element_type=jnp.float32)
        basis = factor if basis is None else basis * factor
        rows = part if rows is None else rows * part
    w = coords[npar:npar + 1]
    low = basis.astype(jnp.bfloat16)
    weighted_rows = (w * rows).astype(jnp.bfloat16)
    gram_ref[...] += lax.dot_general(
        weighted_rows, low, (((1,), (1,)), ((), ())), preferred_element_type=jnp.float32
    )
    if with_weighted:
        wt_refs[0][...] = (w * basis).astype(jnp.bfloat16)


def gram_rows(metas, pick, codes, row0, picked, npar, with_weighted, block=1024):
    rows, samples = metas[0].shape
    per = samples // block
    n_meta = len(metas)
    groups, terms, _ = codes.shape
    width3 = 3 * LEVELS ** GROUP

    def meta_map(k):
        return lambda i, r: (0, jnp.clip(i - k * per, 0, per - 1))

    out_specs = [pl.BlockSpec((picked, terms), lambda i, r: (0, 0))]
    out_shape = [jax.ShapeDtypeStruct((picked, terms), jnp.float32)]
    if with_weighted:
        out_specs.append(pl.BlockSpec((terms, block), lambda i, r: (0, i)))
        out_shape.append(jax.ShapeDtypeStruct((terms, samples), jnp.bfloat16))
    grid_spec = pltpu.PrefetchScalarGridSpec(
        num_scalar_prefetch=1,
        grid=(n_meta * per,),
        in_specs=[pl.BlockSpec((rows, block), meta_map(k)) for k in range(n_meta)] + [
            pl.BlockSpec(pick.shape, lambda i, r: (0, 0, 0)),
            pl.BlockSpec(codes.shape, lambda i, r: (0, 0, 0)),
        ],
        out_specs=out_specs,
        scratch_shapes=[pltpu.VMEM((groups, terms, width3), jnp.bfloat16)],
    )
    kernel = functools.partial(
        gram_kernel, npar=npar, n_meta=n_meta, per=per, picked=picked, with_weighted=with_weighted
    )
    return pl.pallas_call(
        kernel,
        grid_spec=grid_spec,
        out_shape=out_shape,
        compiler_params=pltpu.CompilerParams(
            dimension_semantics=("arbitrary",), vmem_limit_bytes=48 * 1024 * 1024
        ),
    )(row0, *metas, pick, codes)


def moment_kernel(w_ref, *refs, scale):
    p_refs, o_ref = refs[:-1], refs[-1]
    cap = p_refs[0].shape[0]
    acc = None
    for k, p_ref in enumerate(p_refs):
        part = jnp.dot(w_ref[:, k * cap:(k + 1) * cap], p_ref[...], preferred_element_type=jnp.float32)
        acc = part if acc is None else acc + part
    o_ref[...] = acc * scale


def moment_sums(weighted_t, profiles, scale, block=256):
    terms, samples = weighted_t.shape
    cap, q = profiles[0].shape
    return pl.pallas_call(
        functools.partial(moment_kernel, scale=scale),
        grid=(terms // block,),
        in_specs=[pl.BlockSpec((block, samples), lambda i: (i, 0))]
        + [pl.BlockSpec((cap, q), lambda i: (0, 0)) for _ in profiles],
        out_specs=pl.BlockSpec((block, q), lambda i: (i, 0)),
        out_shape=jax.ShapeDtypeStruct((terms, q), jnp.float32),
        compiler_params=pltpu.CompilerParams(
            dimension_semantics=("arbitrary",), vmem_limit_bytes=48 * 1024 * 1024
        ),
    )(weighted_t, *profiles)


def exchange(blocks, groups):
    if groups & (groups - 1):
        got = lax.all_to_all(blocks, "elem", 0, 0, tiled=True)
        return [got[t] for t in range(groups)]
    got = [blocks[0]]
    for m in range(1, groups):
        got.append(lax.ppermute(blocks[m], "elem", [(i, i ^ m) for i in range(groups)]))
    return got


def partners(groups):
    if groups & (groups - 1):
        return jnp.arange(groups, dtype=jnp.int32)
    return lax.axis_index("elem") ^ jnp.arange(groups, dtype=jnp.int32)


def on_device(params, profiles, weights, destinations, table):
    groups = lax.axis_size("elem")
    members = lax.axis_size("grp")
    samples = destinations.shape[0]
    cap = samples // 2
    scale = 1.0 / (members * samples)

    mine = destinations[:, None] == partners(groups)[None, :]
    idx = jnp.arange(samples, dtype=jnp.int32)
    earlier = (idx[:, None] > idx[None, :]).astype(jnp.bfloat16)
    counts = jnp.dot(earlier, mine.astype(jnp.bfloat16), preferred_element_type=jnp.float32)
    slot = jnp.sum(jnp.where(mine, counts, 0.0), axis=1).astype(jnp.int32)
    sel = mine.T[:, None, :] & (slot[None, None, :] == jnp.arange(cap, dtype=jnp.int32)[None, :, None])
    sel = sel.astype(jnp.bfloat16)

    prof_c = jnp.einsum("eis,sq->eiq", sel, profiles, preferred_element_type=jnp.float32).astype(jnp.bfloat16)
    npar = params.shape[0]
    rows = -(-(npar + 1) // 16) * 16
    meta = jnp.concatenate(
        [params, weights[None, :], jnp.zeros((rows - npar - 1, samples), params.dtype)], axis=0
    )
    meta_c = jnp.einsum("eis,js->eji", sel, meta, preferred_element_type=jnp.float32).astype(jnp.bfloat16)
    meta_r = jnp.stack(exchange(meta_c, groups))
    prof_r = exchange(prof_c, groups)

    q = profiles.shape[1]
    terms = table.shape[0]
    slots = groups * cap
    meta_r = jnp.transpose(meta_r, (1, 0, 2)).reshape(rows, slots)

    me = lax.axis_index("grp")
    core = me % 2
    chip = me // 2
    pairs = members // 2
    own_rows = terms // members
    others = [
        lax.ppermute(meta_r, "grp", [(i, (i + 2 * k) % members) for i in range(members)])
        for k in range(1, pairs)
    ]
    codes, pick = term_maps(table, rows)
    row0 = (chip * 2 * own_rows).astype(jnp.int32).reshape(1)
    gram_own, weighted_t = gram_rows([meta_r], pick, codes, row0, 2 * own_rows, npar, True)
    moment_part = moment_sums(weighted_t, prof_r, scale)
    blocks = moment_part.reshape(pairs, 2, own_rows, q)
    mine = lax.dynamic_index_in_dim(blocks, core, axis=1, keepdims=False)
    theirs = lax.dynamic_index_in_dim(blocks, 1 - core, axis=1, keepdims=False)
    swapped = lax.ppermute(theirs, "grp", [(i, i ^ 1) for i in range(members)])
    (gram_oth,) = gram_rows(others[:1], pick, codes, row0, 2 * own_rows, npar, False)
    chip_sum = mine + swapped
    moment_rows = lax.dynamic_index_in_dim(chip_sum, chip, axis=0, keepdims=False)
    arrived = [
        lax.ppermute(
            lax.dynamic_index_in_dim(chip_sum, (chip + k) % pairs, axis=0, keepdims=False),
            "grp", [(i, (i + 2 * k) % members) for i in range(members)])
        for k in range(1, pairs)
    ]
    if len(others) > 1:
        (gram_b,) = gram_rows(others[1:], pick, codes, row0, 2 * own_rows, npar, False)
        gram_oth = gram_oth + gram_b
    for block in arrived:
        moment_rows = moment_rows + block
    gram_chip = gram_own + gram_oth
    keep = lax.dynamic_slice_in_dim(gram_chip, core * own_rows, own_rows, axis=0)
    send = lax.dynamic_slice_in_dim(gram_chip, (1 - core) * own_rows, own_rows, axis=0)
    recv = lax.ppermute(send, "grp", [(i, i ^ 1) for i in range(members)])
    gram_out = (keep + recv) * scale
    return (gram_out[None], moment_rows[None])


def solution(mesh):
    in_specs = (
        P(None, ("elem", "grp")),
        P(("elem", "grp"), None),
        P(("elem", "grp")),
        P(("elem", "grp")),
        P(),
    )
    out_specs = (P("elem", "grp", None), P("elem", "grp", None))

    return jax.shard_map(on_device, mesh=mesh, in_specs=in_specs, out_specs=out_specs, check_vma=False)
```

```python
import functools

import numpy as np
import jax
import jax.numpy as jnp
from jax import lax
from jax.sharding import PartitionSpec as P
from jax.experimental import pallas as pl
from jax.experimental.pallas import tpu as pltpu

LEVELS = 4
GROUP = 3


def split3(x):
    hi = x.astype(jnp.bfloat16)
    rest = x - hi.astype(jnp.float32)
    mid = rest.astype(jnp.bfloat16)
    lo = (rest - mid.astype(jnp.float32)).astype(jnp.bfloat16)
    return jnp.concatenate([hi, mid, lo], axis=0)


def term_maps(table, rows):
    npar = table.shape[1]
    width = LEVELS ** GROUP
    n_groups = -(-npar // GROUP)
    codes = []
    for start in range(0, n_groups * GROUP, GROUP):
        code = jnp.zeros((table.shape[0],), jnp.int32)
        for j in range(start, start + GROUP):
            code = code * LEVELS + (table[:, j] if j < npar else 0)
        codes.append(code)
    pick = np.zeros((GROUP, n_groups * width, 3 * LEVELS * rows), np.float32)
    for g in range(n_groups):
        for c in range(width):
            for pos in range(GROUP):
                j = g * GROUP + pos
                degree = (c // LEVELS ** (GROUP - 1 - pos)) % LEVELS
                col = degree * rows + j if j < npar else 0
                for piece in range(3):
                    pick[pos, g * width + c, piece * LEVELS * rows + col] = 1.0
    return jnp.stack(codes)[:, :, None], jnp.asarray(pick, jnp.bfloat16)


def gram_kernel(row0_ref, *refs, npar, n_meta, per, picked, with_weighted):
    metas = refs[:n_meta]
    pick_ref, code_ref, gram_ref = refs[n_meta:n_meta + 3]
    wt_refs = refs[n_meta + 3:-1] if with_weighted else ()
    oh_ref = refs[-1]
    step = pl.program_id(0)
    groups, _, width3 = oh_ref.shape
    width = width3 // 3

    @pl.when(step == 0)
    def _():
        gram_ref[...] = jnp.zeros_like(gram_ref)
        lanes = lax.broadcasted_iota(jnp.int32, (1, width3), 1) % width
        for g in range(groups):
            oh_ref[g] = (code_ref[g] == lanes).astype(jnp.bfloat16)

    m = metas[0][...]
    for k in range(1, n_meta):
        m = jnp.where(step >= k * per, metas[k][...], m)
    coords = m.astype(jnp.float32)
    values = [jnp.ones_like(coords), coords]
    for degree in range(1, LEVELS - 1):
        nxt = ((2.0 * degree + 1.0) * coords * values[-1] - degree * values[-2]) / (degree + 1.0)
        values.append(nxt)
    stacked = jnp.concatenate(
        [values[d] * float(np.sqrt(np.float32(2 * d + 1))) for d in range(LEVELS)], axis=0
    )
    pieces = split3(stacked)
    combos = None
    for pos in range(pick_ref.shape[0]):
        factor = jnp.dot(pick_ref[pos], pieces, preferred_element_type=jnp.float32)
        combos = factor if combos is None else combos * factor
    row0 = pl.multiple_of(row0_ref[0], picked)
    basis = None
    rows = None
    for g in range(groups):
        piece = split3(combos[g * width:(g + 1) * width])
        factor = jnp.dot(oh_ref[g], piece, preferred_element_type=jnp.float32)
        part = jnp.dot(oh_ref[g, pl.ds(row0, picked), :], piece, preferred_element_type=jnp.float32)
        basis = factor if basis is None else basis * factor
        rows = part if rows is None else rows * part
    w = coords[npar:npar + 1]
    low = basis.astype(jnp.bfloat16)
    weighted_rows = (w * rows).astype(jnp.bfloat16)
    gram_ref[...] += lax.dot_general(
        weighted_rows, low, (((1,), (1,)), ((), ())), preferred_element_type=jnp.float32
    )
    if with_weighted:
        wt_refs[0][...] = (w * basis).astype(jnp.bfloat16)


def gram_rows(metas, pick, codes, row0, picked, npar, with_weighted, block=1024):
    rows, samples = metas[0].shape
    per = samples // block
    n_meta = len(metas)
    groups, terms, _ = codes.shape
    width3 = 3 * LEVELS ** GROUP

    def meta_map(k):
        return lambda i, r: (0, jnp.clip(i - k * per, 0, per - 1))

    out_specs = [pl.BlockSpec((picked, terms), lambda i, r: (0, 0))]
    out_shape = [jax.ShapeDtypeStruct((picked, terms), jnp.float32)]
    if with_weighted:
        out_specs.append(pl.BlockSpec((terms, block), lambda i, r: (0, i)))
        out_shape.append(jax.ShapeDtypeStruct((terms, samples), jnp.bfloat16))
    grid_spec = pltpu.PrefetchScalarGridSpec(
        num_scalar_prefetch=1,
        grid=(n_meta * per,),
        in_specs=[pl.BlockSpec((rows, block), meta_map(k)) for k in range(n_meta)] + [
            pl.BlockSpec(pick.shape, lambda i, r: (0, 0, 0)),
            pl.BlockSpec(codes.shape, lambda i, r: (0, 0, 0)),
        ],
        out_specs=out_specs,
        scratch_shapes=[pltpu.VMEM((groups, terms, width3), jnp.bfloat16)],
    )
    kernel = functools.partial(
        gram_kernel, npar=npar, n_meta=n_meta, per=per, picked=picked, with_weighted=with_weighted
    )
    return pl.pallas_call(
        kernel,
        grid_spec=grid_spec,
        out_shape=out_shape,
        compiler_params=pltpu.CompilerParams(
            dimension_semantics=("arbitrary",), vmem_limit_bytes=48 * 1024 * 1024
        ),
    )(row0, *metas, pick, codes)


def moment_kernel(w_ref, *refs, scale):
    p_refs, o_ref = refs[:-1], refs[-1]
    cap = p_refs[0].shape[0]
    acc = None
    for k, p_ref in enumerate(p_refs):
        part = jnp.dot(w_ref[:, k * cap:(k + 1) * cap], p_ref[...], preferred_element_type=jnp.float32)
        acc = part if acc is None else acc + part
    o_ref[...] = acc * scale


def moment_sums(weighted_t, profiles, scale, block=256):
    terms, samples = weighted_t.shape
    cap, q = profiles[0].shape
    return pl.pallas_call(
        functools.partial(moment_kernel, scale=scale),
        grid=(terms // block,),
        in_specs=[pl.BlockSpec((block, samples), lambda i: (i, 0))]
        + [pl.BlockSpec((cap, q), lambda i: (0, 0)) for _ in profiles],
        out_specs=pl.BlockSpec((block, q), lambda i: (i, 0)),
        out_shape=jax.ShapeDtypeStruct((terms, q), jnp.float32),
        compiler_params=pltpu.CompilerParams(
            dimension_semantics=("arbitrary",), vmem_limit_bytes=48 * 1024 * 1024
        ),
    )(weighted_t, *profiles)


def exchange(blocks, groups):
    if groups & (groups - 1):
        got = lax.all_to_all(blocks, "elem", 0, 0, tiled=True)
        return [got[t] for t in range(groups)]
    got = [blocks[0]]
    for m in range(1, groups):
        got.append(lax.ppermute(blocks[m], "elem", [(i, i ^ m) for i in range(groups)]))
    return got


def partners(groups):
    if groups & (groups - 1):
        return jnp.arange(groups, dtype=jnp.int32)
    return lax.axis_index("elem") ^ jnp.arange(groups, dtype=jnp.int32)


def on_device(params, profiles, weights, destinations, table):
    groups = lax.axis_size("elem")
    members = lax.axis_size("grp")
    samples = destinations.shape[0]
    cap = samples // 2
    scale = 1.0 / (members * samples)

    mine = destinations[:, None] == partners(groups)[None, :]
    idx = jnp.arange(samples, dtype=jnp.int32)
    earlier = (idx[:, None] > idx[None, :]).astype(jnp.bfloat16)
    counts = jnp.dot(earlier, mine.astype(jnp.bfloat16), preferred_element_type=jnp.float32)
    slot = jnp.sum(jnp.where(mine, counts, 0.0), axis=1).astype(jnp.int32)
    sel = mine.T[:, None, :] & (slot[None, None, :] == jnp.arange(cap, dtype=jnp.int32)[None, :, None])
    sel = sel.astype(jnp.bfloat16)

    prof_c = jnp.einsum("eis,sq->eiq", sel, profiles, preferred_element_type=jnp.float32).astype(jnp.bfloat16)
    npar = params.shape[0]
    rows = -(-(npar + 1) // 16) * 16
    meta = jnp.concatenate(
        [params, weights[None, :], jnp.zeros((rows - npar - 1, samples), params.dtype)], axis=0
    )
    meta_c = jnp.einsum("eis,js->eji", sel, meta, preferred_element_type=jnp.float32).astype(jnp.bfloat16)
    meta_r = jnp.stack(exchange(meta_c, groups))
    prof_r = exchange(prof_c, groups)

    q = profiles.shape[1]
    terms = table.shape[0]
    slots = groups * cap
    meta_r = jnp.transpose(meta_r, (1, 0, 2)).reshape(rows, slots)

    me = lax.axis_index("grp")
    core = me % 2
    chip = me // 2
    pairs = members // 2
    own_rows = terms // members
    others = [
        lax.ppermute(meta_r, "grp", [(i, (i + 2 * k) % members) for i in range(members)])
        for k in range(1, pairs)
    ]
    codes, pick = term_maps(table, rows)
    row0 = (chip * 2 * own_rows).astype(jnp.int32).reshape(1)
    gram_own, weighted_t = gram_rows([meta_r], pick, codes, row0, 2 * own_rows, npar, True)
    moment_part = moment_sums(weighted_t, prof_r, scale)
    blocks = moment_part.reshape(pairs, 2, own_rows, q)
    mine = lax.dynamic_index_in_dim(blocks, core, axis=1, keepdims=False)
    theirs = lax.dynamic_index_in_dim(blocks, 1 - core, axis=1, keepdims=False)
    swapped = lax.ppermute(theirs, "grp", [(i, i ^ 1) for i in range(members)])
    chip_sum = mine + swapped
    moment_rows = lax.dynamic_index_in_dim(chip_sum, chip, axis=0, keepdims=False)
    arrived = [
        lax.ppermute(
            lax.dynamic_index_in_dim(chip_sum, (chip + k) % pairs, axis=0, keepdims=False),
            "grp", [(i, (i + 2 * k) % members) for i in range(members)])
        for k in range(1, pairs)
    ]
    (gram_oth,) = gram_rows(others, pick, codes, row0, 2 * own_rows, npar, False)
    for block in arrived:
        moment_rows = moment_rows + block
    gram_chip = gram_own + gram_oth
    keep = lax.dynamic_slice_in_dim(gram_chip, core * own_rows, own_rows, axis=0)
    send = lax.dynamic_slice_in_dim(gram_chip, (1 - core) * own_rows, own_rows, axis=0)
    recv = lax.ppermute(send, "grp", [(i, i ^ 1) for i in range(members)])
    gram_out = (keep + recv) * scale
    return (gram_out[None], moment_rows[None])


def solution(mesh):
    in_specs = (
        P(None, ("elem", "grp")),
        P(("elem", "grp"), None),
        P(("elem", "grp")),
        P(("elem", "grp")),
        P(),
    )
    out_specs = (P("elem", "grp", None), P("elem", "grp", None))

    return jax.shard_map(on_device, mesh=mesh, in_specs=in_specs, out_specs=out_specs, check_vma=False)
```

```python
import functools

import numpy as np
import jax
import jax.numpy as jnp
from jax import lax
from jax.sharding import PartitionSpec as P
from jax.experimental import pallas as pl
from jax.experimental.pallas import tpu as pltpu

LEVELS = 4
GROUP = 3


def split3(x):
    hi = x.astype(jnp.bfloat16)
    rest = x - hi.astype(jnp.float32)
    mid = rest.astype(jnp.bfloat16)
    lo = (rest - mid.astype(jnp.float32)).astype(jnp.bfloat16)
    return jnp.concatenate([hi, mid, lo], axis=0)


def term_maps(table, rows):
    npar = table.shape[1]
    width = LEVELS ** GROUP
    n_groups = -(-npar // GROUP)
    codes = []
    for start in range(0, n_groups * GROUP, GROUP):
        code = jnp.zeros((table.shape[0],), jnp.int32)
        for j in range(start, start + GROUP):
            code = code * LEVELS + (table[:, j] if j < npar else 0)
        codes.append(code)
    pick = np.zeros((GROUP, n_groups * width, 3 * LEVELS * rows), np.float32)
    for g in range(n_groups):
        for c in range(width):
            for pos in range(GROUP):
                j = g * GROUP + pos
                degree = (c // LEVELS ** (GROUP - 1 - pos)) % LEVELS
                col = degree * rows + j if j < npar else 0
                for piece in range(3):
                    pick[pos, g * width + c, piece * LEVELS * rows + col] = 1.0
    return jnp.stack(codes)[:, :, None], jnp.asarray(pick, jnp.bfloat16)


def gram_kernel(row0_ref, *refs, npar, n_meta, per, picked, with_weighted, with_init):
    metas = refs[:n_meta]
    pick_ref, code_ref = refs[n_meta:n_meta + 2]
    rest = refs[n_meta + 2:]
    init_refs = rest[:1] if with_init else ()
    gram_ref = rest[len(init_refs)]
    wt_refs = rest[len(init_refs) + 1:-1] if with_weighted else ()
    oh_ref = refs[-1]
    step = pl.program_id(0)
    groups, _, width3 = oh_ref.shape
    width = width3 // 3

    @pl.when(step == 0)
    def _():
        gram_ref[...] = init_refs[0][...] if with_init else jnp.zeros_like(gram_ref)
        lanes = lax.broadcasted_iota(jnp.int32, (1, width3), 1) % width
        for g in range(groups):
            oh_ref[g] = (code_ref[g] == lanes).astype(jnp.bfloat16)

    m = metas[0][...]
    for k in range(1, n_meta):
        m = jnp.where(step >= k * per, metas[k][...], m)
    coords = m.astype(jnp.float32)
    values = [jnp.ones_like(coords), coords]
    for degree in range(1, LEVELS - 1):
        nxt = ((2.0 * degree + 1.0) * coords * values[-1] - degree * values[-2]) / (degree + 1.0)
        values.append(nxt)
    stacked = jnp.concatenate(
        [values[d] * float(np.sqrt(np.float32(2 * d + 1))) for d in range(LEVELS)], axis=0
    )
    pieces = split3(stacked)
    combos = None
    for pos in range(pick_ref.shape[0]):
        factor = jnp.dot(pick_ref[pos], pieces, preferred_element_type=jnp.float32)
        combos = factor if combos is None else combos * factor
    row0 = pl.multiple_of(row0_ref[0], picked)
    basis = None
    rows = None
    for g in range(groups):
        piece = split3(combos[g * width:(g + 1) * width])
        factor = jnp.dot(oh_ref[g], piece, preferred_element_type=jnp.float32)
        part = jnp.dot(oh_ref[g, pl.ds(row0, picked), :], piece, preferred_element_type=jnp.float32)
        basis = factor if basis is None else basis * factor
        rows = part if rows is None else rows * part
    w = coords[npar:npar + 1]
    low = basis.astype(jnp.bfloat16)
    weighted_rows = (w * rows).astype(jnp.bfloat16)
    gram_ref[...] += lax.dot_general(
        weighted_rows, low, (((1,), (1,)), ((), ())), preferred_element_type=jnp.float32
    )
    if with_weighted:
        wt_refs[0][...] = (w * basis).astype(jnp.bfloat16)


def gram_rows(metas, pick, codes, row0, picked, npar, with_weighted, block=1024, init=None):
    rows, samples = metas[0].shape
    per = samples // block
    n_meta = len(metas)
    groups, terms, _ = codes.shape
    width3 = 3 * LEVELS ** GROUP

    def meta_map(k):
        return lambda i, r: (0, jnp.clip(i - k * per, 0, per - 1))

    out_specs = [pl.BlockSpec((picked, terms), lambda i, r: (0, 0))]
    out_shape = [jax.ShapeDtypeStruct((picked, terms), jnp.float32)]
    if with_weighted:
        out_specs.append(pl.BlockSpec((terms, block), lambda i, r: (0, i)))
        out_shape.append(jax.ShapeDtypeStruct((terms, samples), jnp.bfloat16))
    grid_spec = pltpu.PrefetchScalarGridSpec(
        num_scalar_prefetch=1,
        grid=(n_meta * per,),
        in_specs=[pl.BlockSpec((rows, block), meta_map(k)) for k in range(n_meta)] + [
            pl.BlockSpec(pick.shape, lambda i, r: (0, 0, 0)),
            pl.BlockSpec(codes.shape, lambda i, r: (0, 0, 0)),
        ] + ([pl.BlockSpec((picked, terms), lambda i, r: (0, 0))] if init is not None else []),
        out_specs=out_specs,
        scratch_shapes=[pltpu.VMEM((groups, terms, width3), jnp.bfloat16)],
    )
    kernel = functools.partial(
        gram_kernel, npar=npar, n_meta=n_meta, per=per, picked=picked, with_weighted=with_weighted,
        with_init=init is not None,
    )
    return pl.pallas_call(
        kernel,
        grid_spec=grid_spec,
        out_shape=out_shape,
        compiler_params=pltpu.CompilerParams(
            dimension_semantics=("arbitrary",), vmem_limit_bytes=48 * 1024 * 1024
        ),
    )(row0, *metas, pick, codes, *([init] if init is not None else []))


def moment_kernel(w_ref, *refs, scale):
    p_refs, o_ref = refs[:-1], refs[-1]
    cap = p_refs[0].shape[0]
    acc = None
    for k, p_ref in enumerate(p_refs):
        part = jnp.dot(w_ref[:, k * cap:(k + 1) * cap], p_ref[...], preferred_element_type=jnp.float32)
        acc = part if acc is None else acc + part
    o_ref[...] = acc * scale


def moment_sums(weighted_t, profiles, scale, block=256):
    terms, samples = weighted_t.shape
    cap, q = profiles[0].shape
    return pl.pallas_call(
        functools.partial(moment_kernel, scale=scale),
        grid=(terms // block,),
        in_specs=[pl.BlockSpec((block, samples), lambda i: (i, 0))]
        + [pl.BlockSpec((cap, q), lambda i: (0, 0)) for _ in profiles],
        out_specs=pl.BlockSpec((block, q), lambda i: (i, 0)),
        out_shape=jax.ShapeDtypeStruct((terms, q), jnp.float32),
        compiler_params=pltpu.CompilerParams(
            dimension_semantics=("arbitrary",), vmem_limit_bytes=48 * 1024 * 1024
        ),
    )(weighted_t, *profiles)


def exchange(blocks, groups):
    if groups & (groups - 1):
        got = lax.all_to_all(blocks, "elem", 0, 0, tiled=True)
        return [got[t] for t in range(groups)]
    got = [blocks[0]]
    for m in range(1, groups):
        got.append(lax.ppermute(blocks[m], "elem", [(i, i ^ m) for i in range(groups)]))
    return got


def partners(groups):
    if groups & (groups - 1):
        return jnp.arange(groups, dtype=jnp.int32)
    return lax.axis_index("elem") ^ jnp.arange(groups, dtype=jnp.int32)


def on_device(params, profiles, weights, destinations, table):
    groups = lax.axis_size("elem")
    members = lax.axis_size("grp")
    samples = destinations.shape[0]
    cap = samples // 2
    scale = 1.0 / (members * samples)

    mine = destinations[:, None] == partners(groups)[None, :]
    idx = jnp.arange(samples, dtype=jnp.int32)
    earlier = (idx[:, None] > idx[None, :]).astype(jnp.bfloat16)
    counts = jnp.dot(earlier, mine.astype(jnp.bfloat16), preferred_element_type=jnp.float32)
    slot = jnp.sum(jnp.where(mine, counts, 0.0), axis=1).astype(jnp.int32)
    sel = mine.T[:, None, :] & (slot[None, None, :] == jnp.arange(cap, dtype=jnp.int32)[None, :, None])
    sel = sel.astype(jnp.bfloat16)

    prof_c = jnp.einsum("eis,sq->eiq", sel, profiles, preferred_element_type=jnp.float32).astype(jnp.bfloat16)
    npar = params.shape[0]
    rows = -(-(npar + 1) // 16) * 16
    meta = jnp.concatenate(
        [params, weights[None, :], jnp.zeros((rows - npar - 1, samples), params.dtype)], axis=0
    )
    meta_c = jnp.einsum("eis,js->eji", sel, meta, preferred_element_type=jnp.float32).astype(jnp.bfloat16)
    meta_r = jnp.stack(exchange(meta_c, groups))
    prof_r = exchange(prof_c, groups)

    q = profiles.shape[1]
    terms = table.shape[0]
    slots = groups * cap
    meta_r = jnp.transpose(meta_r, (1, 0, 2)).reshape(rows, slots)

    me = lax.axis_index("grp")
    core = me % 2
    chip = me // 2
    pairs = members // 2
    own_rows = terms // members
    others = [
        lax.ppermute(meta_r, "grp", [(i, (i + 2 * k) % members) for i in range(members)])
        for k in range(1, pairs)
    ]
    codes, pick = term_maps(table, rows)
    row0 = (chip * 2 * own_rows).astype(jnp.int32).reshape(1)
    gram_own, weighted_t = gram_rows([meta_r], pick, codes, row0, 2 * own_rows, npar, True)
    moment_part = moment_sums(weighted_t, prof_r, scale)
    blocks = moment_part.reshape(pairs, 2, own_rows, q)
    mine = lax.dynamic_index_in_dim(blocks, core, axis=1, keepdims=False)
    theirs = lax.dynamic_index_in_dim(blocks, 1 - core, axis=1, keepdims=False)
    swapped = lax.ppermute(theirs, "grp", [(i, i ^ 1) for i in range(members)])
    chip_sum = mine + swapped
    moment_rows = lax.dynamic_index_in_dim(chip_sum, chip, axis=0, keepdims=False)
    arrived = [
        lax.ppermute(
            lax.dynamic_index_in_dim(chip_sum, (chip + k) % pairs, axis=0, keepdims=False),
            "grp", [(i, (i + 2 * k) % members) for i in range(members)])
        for k in range(1, pairs)
    ]
    (gram_chip,) = gram_rows(others, pick, codes, row0, 2 * own_rows, npar, False, init=gram_own)
    for block in arrived:
        moment_rows = moment_rows + block
    keep = lax.dynamic_slice_in_dim(gram_chip, core * own_rows, own_rows, axis=0)
    send = lax.dynamic_slice_in_dim(gram_chip, (1 - core) * own_rows, own_rows, axis=0)
    recv = lax.ppermute(send, "grp", [(i, i ^ 1) for i in range(members)])
    gram_out = (keep + recv) * scale
    return (gram_out[None], moment_rows[None])


def solution(mesh):
    in_specs = (
        P(None, ("elem", "grp")),
        P(("elem", "grp"), None),
        P(("elem", "grp")),
        P(("elem", "grp")),
        P(),
    )
    out_specs = (P("elem", "grp", None), P("elem", "grp", None))

    return jax.shard_map(on_device, mesh=mesh, in_specs=in_specs, out_specs=out_specs, check_vma=False)
```
